32 devices in a mesh: groups: 2 (over y), area: 4 (over z), neuron: 4 (over x, core).
Axes of the slice: x: 2, y: 2, z: 4, core: 2. Of those that a mesh axis runs over, the one named last changes fastest.
Arguments:
- window: bfloat16 [32, 16, 32768], P(None, 'groups', ('area', 'neuron')), parts along dimension 1, may hold values from -6 to 6
- err_grad: float32 [16, 16, 32768], P(None, 'groups', ('area', 'neuron')), parts along dimension 1, may hold values from -6 to 6
- surrogate: float32 [16, 16, 32768], P(None, 'groups', ('area', 'neuron')), parts along dimension 1, may hold values from 0 to 0.5
- lv_end: float32 [16, 32768], P('groups', ('area', 'neuron')), parts along dimension 0, may hold values from -6 to 6
- la_end: float32 [16, 32768], P('groups', ('area', 'neuron')), parts along dimension 0, may hold values from -6 to 6
- alpha: float32 [32768], P(('area', 'neuron')), may hold values from 0.8 to 0.99
- rho: float32 [32768], P(('area', 'neuron')), may hold values from 0.9 to 0.999
- beta: float32 [32768], P(('area', 'neuron')), may hold values from 0.3 to 2
- weights: bfloat16 [4, 4, 64, 4, 128, 128], P(None, 'area', 'neuron'), may hold values from -0.25 to 0.25
- block_index: int32 [4, 4, 64, 4], P(None, 'area', 'neuron'), may hold values from 0 to 63, as said below
- delays: int32 [4, 4], replicated, may hold values from 16 to 31, as said below
Outputs:
- cur_adjoint: bfloat16 [16, 16, 32768], P(None, 'groups', ('area', 'neuron')), parts along dimension 1
- lv_start: float32 [16, 32768], P('groups', ('area', 'neuron')), parts along dimension 0
- la_start: float32 [16, 32768], P('groups', ('area', 'neuron')), parts along dimension 0
The draws below stay inside these ranges and needn't reach their ends.
There are 2 independent parts, one for each index of `groups`. The reference program is written for one: setup_inputs(seed, part) draws one part's arguments, and reference() takes and returns one part's arrays. A program takes and returns all parts, laid end to end along the dimension named above; an argument that names none is the same for every part. Nothing has to cross between parts.
Inputs may be any that keep to these rules, and one draw needn't show every extreme that they name: `delays`: every entry lies in 16 to 31 and both ends occur. `block_index`: both ends occur.
All inputs are finite; a program needn't handle non-finite values.
Results may differ from the reference program's by a relative error of at most 0.001.
Values may be sent and summed in bfloat16 or wider, within the bound.
No kernel may reach another device: no remote copies, remote signals or barrier semaphores. Data moves between devices by JAX's collectives and lax.ppermute only.
A program may use at most 64 MiB of HBM per device.

```python
import math
import jax
import jax.numpy as jnp
from jax import lax

K = 16
B = 8
BLK = 128
NNZ = 4
ROUNDS = 4
AREAS = 4
NA = 8192
NBA = 64
NEUR = 32768
N_AREA = 4


def draw_block_index(key, part):
    values = jax.random.randint(jax.random.fold_in(key, 11), (ROUNDS, AREAS, NBA, NNZ), 0, NBA)
    values = values.at[0, 0, 0, 0].set(NBA - 1)
    values = values.at[0, 0, 0, 1].set(0)
    return values.astype(jnp.int32)


def draw_delays(key, part):
    values = jax.random.randint(jax.random.fold_in(key, 23), (ROUNDS, AREAS), K, 2 * K)
    values = values.at[0, 0].set(2 * K - 1)
    values = values.at[0, 1].set(K)
    return values.astype(jnp.int32)


def level_of(own_key, dims, pieces, least, largest):
    def one(dim, parts):
        draws = jax.random.uniform(jax.random.fold_in(jax.random.fold_in(own_key, 6), dim), (parts,), jnp.float32, least / len(pieces), largest / len(pieces))
        return jnp.repeat(jnp.exp(draws), dims[dim] // parts).reshape((-1,) + (1,) * (len(dims) - dim - 1))

    gain = one(*pieces[0])
    for cut in pieces[1:]:
        gain = gain * one(*cut)
    return gain


def scatter_about(own_key, extent, scale, most, pieces=(), held_as=jnp.bfloat16):
    values = jax.random.normal(own_key, extent, jnp.float32) * scale
    if len(pieces) > 0:
        values = level_of(own_key, extent, pieces, -0.22, 0.18) * values
    return jnp.clip(values, min=-most, max=most).astype(held_as)


def setup_inputs(seed: int = 0, part: int = 0) -> dict:
    key_list = jax.random.split(jax.random.key(seed), 12)
    part_splits = jax.random.split(jax.random.fold_in(key_list[11], part), 12)
    return {
        "window": scatter_about(part_splits[0], (2 * K, B, NEUR), 1.0, 6.0, ((2, 16),)),
        "err_grad": scatter_about(part_splits[1], (K, B, NEUR), 1.0, 6.0, ((2, 16),), jnp.float32),
        "surrogate": jnp.clip(0.5 * jax.random.uniform(part_splits[2], (K, B, NEUR), jnp.float32) ** level_of(part_splits[2], (K, B, NEUR), ((2, 16),), -0.2, 0.2), 0.0, 0.5),
        "lv_end": scatter_about(part_splits[3], (B, NEUR), 1.0, 6.0, ((1, 16),), jnp.float32),
        "la_end": scatter_about(part_splits[4], (B, NEUR), 1.0, 6.0, ((1, 16),), jnp.float32),
        "alpha": jnp.clip(jnp.exp(math.log(0.99) - 0.2130932 * jax.random.uniform(key_list[5], (NEUR,), jnp.float32) ** level_of(key_list[5], (NEUR,), ((0, 16),), -0.2, 0.2)), 0.8, 0.99),
        "rho": jnp.clip(jnp.exp(math.log(0.999) - 0.10436005 * jax.random.uniform(key_list[6], (NEUR,), jnp.float32) ** level_of(key_list[6], (NEUR,), ((0, 16),), -0.2, 0.2)), 0.9, 0.999),
        "beta": jnp.clip(jnp.exp(math.log(2.0) - 1.89712 * jax.random.uniform(key_list[7], (NEUR,), jnp.float32) ** level_of(key_list[7], (NEUR,), ((0, 16),), -0.2, 0.2)), 0.3, 2.0),
        "weights": scatter_about(key_list[8], (ROUNDS, AREAS, NBA, NNZ, BLK, BLK), (NNZ * BLK) ** -0.5, 0.25, ((1, 4), (2, 4))),
        "block_index": draw_block_index(jax.random.fold_in(key_list[11], 71), part),
        "delays": draw_delays(jax.random.fold_in(key_list[11], 71), part),
    }


def adjoint_scan(err_grad, surrogate, rec, lv_end, la_end, alpha, rho, beta):
    def step(carry, inputs):
        lv_now, la_now = carry
        error_t, surr_t, rec_t = inputs
        total = error_t + rec_t - lv_now + la_now
        lv_next = alpha * lv_now + surr_t * total
        la_next = rho * la_now - beta * surr_t * total
        return (lv_next, la_next), lv_now.astype(jnp.bfloat16)

    (lv_start, la_start), currents = lax.scan(step, (lv_end, la_end), (err_grad, surrogate, rec), reverse=True)
    return currents, lv_start, la_start


def reference(window, err_grad, surrogate, lv_end, la_end, alpha, rho, beta, weights, block_index, delays):
    levels = N_AREA.bit_length() - 1
    area_ids = jnp.arange(N_AREA, dtype=jnp.int32)
    split = window.reshape(2 * K, B, N_AREA, NA)
    rec = jnp.zeros((N_AREA, K * B, NA), jnp.float32)
    for rnd in range(ROUNDS):
        partners = jnp.bitwise_xor(area_ids, 1 << (rnd % levels))

        def one_area(area):
            partner = partners[area]
            start = (delays[rnd, area] - K).astype(jnp.int32)
            zero = jnp.zeros((), jnp.int32)
            slab = lax.dynamic_slice(split, (start, zero, partner.astype(jnp.int32), zero), (K, B, 1, NA))
            slab = slab.reshape(K * B, NBA, BLK)
            picked = jnp.take(slab, block_index[rnd, area], axis=1)
            blocks = weights[rnd, area]
            out = jnp.einsum("rjkc,jkcd->rjd", picked.astype(jnp.float32), blocks.astype(jnp.float32))
            return out.reshape(K * B, NA)

        rec = rec + lax.map(one_area, area_ids)
    rec = jnp.transpose(rec, (1, 0, 2)).reshape(K, B, N_AREA * NA)
    return adjoint_scan(err_grad, surrogate, rec, lv_end, la_end, alpha, rho, beta)
```

```python
import jax
import jax.numpy as jnp
from jax import lax
from jax.sharding import PartitionSpec as P


def swap(value, axis, mask):
    pairs = [(source, source ^ mask) for source in range(lax.axis_size(axis))]
    return lax.ppermute(value, axis, pairs)


def gather_neuron(piece):
    size = lax.axis_size("neuron")
    bits = size.bit_length() - 1
    held = piece[None]
    for bit in reversed(range(bits)):
        other = swap(held, "neuron", 1 << bit)
        held = jnp.concatenate([held, other], axis=0)
    return held


def relative_position(n, me, bits):
    d = n ^ me
    pos = jnp.zeros_like(d)
    for s, bit in enumerate(reversed(range(bits))):
        pos = pos | (((d >> bit) & 1) << s)
    return pos


def adjoint_scan(err_grad, surrogate, rec, lv_end, la_end, alpha, rho, beta):
    steps = err_grad.shape[0]
    lv_now, la_now = lv_end, la_end
    currents = [None] * steps
    for t in reversed(range(steps)):
        total = err_grad[t] + rec[t] - lv_now + la_now
        currents[t] = lv_now.astype(jnp.bfloat16)
        lv_next = alpha * lv_now + surrogate[t] * total
        la_next = rho * la_now - beta * surrogate[t] * total
        lv_now, la_now = lv_next, la_next
    return (jnp.stack(currents), lv_now, la_now)


def per_device(
    window, err_grad, surrogate, lv_end, la_end, alpha, rho, beta, weights, block_index, delays
):
    steps = err_grad.shape[0]
    batch = err_grad.shape[1]
    local_neurons = err_grad.shape[2]
    block_side = weights.shape[-1]
    local_blocks = local_neurons // block_side
    rounds = weights.shape[0]
    levels = lax.axis_size("area").bit_length() - 1
    nbits = lax.axis_size("neuron").bit_length() - 1
    me_area = lax.axis_index("area")
    me_neuron = lax.axis_index("neuron")
    rec = jnp.zeros((steps * batch, local_neurons), jnp.float32)
    for rnd in range(rounds):
        mask = 1 << (rnd % levels)
        start = delays[rnd, me_area ^ mask] - steps
        piece = lax.dynamic_slice_in_dim(window, start, steps, 0)
        arrived = swap(piece, "area", mask)
        panel = gather_neuron(arrived)
        flat = panel.reshape(panel.shape[0], steps * batch, local_blocks, block_side)
        flat = jnp.moveaxis(flat, 1, 0).reshape(steps * batch, -1, block_side)
        idx = block_index[rnd, 0]
        owner = idx // local_blocks
        pos = relative_position(owner, me_neuron, nbits) * local_blocks + idx % local_blocks
        picked = jnp.take(flat, pos, axis=1)
        contrib = jnp.einsum(
            "rjkc,jkcd->rjd", picked, weights[rnd, 0], preferred_element_type=jnp.float32
        )
        rec = rec + contrib.reshape(steps * batch, local_neurons)
    rec = rec.reshape(steps, batch, local_neurons)
    return adjoint_scan(err_grad, surrogate, rec, lv_end, la_end, alpha, rho, beta)


def solution(mesh):
    placed = (
        P(None, "groups", ("area", "neuron")),
        P(None, "groups", ("area", "neuron")),
        P(None, "groups", ("area", "neuron")),
        P("groups", ("area", "neuron")),
        P("groups", ("area", "neuron")),
        P(("area", "neuron")),
        P(("area", "neuron")),
        P(("area", "neuron")),
        P(None, "area", "neuron", None, None, None),
        P(None, "area", "neuron", None),
        P(),
    )
    return jax.shard_map(
        per_device,
        mesh=mesh,
        in_specs=placed,
        out_specs=(
            P(None, "groups", ("area", "neuron")),
            P("groups", ("area", "neuron")),
            P("groups", ("area", "neuron")),
        ),
        check_vma=False,
    )
```

```python
import functools

import jax
import jax.numpy as jnp
from jax import lax
from jax.experimental import pallas as pl
from jax.experimental.pallas import tpu as pltpu
from jax.sharding import PartitionSpec as P


def swap(value, axis, mask):
    pairs = [(source, source ^ mask) for source in range(lax.axis_size(axis))]
    return lax.ppermute(value, axis, pairs)


def gather_neuron(piece):
    size = lax.axis_size("neuron")
    bits = size.bit_length() - 1
    held = [piece]
    for bit in reversed(range(bits)):
        held = held + [swap(chunk, "neuron", 1 << bit) for chunk in held]
    return held


def relative_position(n, me, bits):
    d = n ^ me
    pos = jnp.zeros_like(d)
    for s, bit in enumerate(reversed(range(bits))):
        pos = pos | (((d >> bit) & 1) << s)
    return pos


def round_kernel(pos_ref, *refs, n_chunks, local_blocks, nnz, first):
    chunk_refs = refs[:n_chunks]
    w_ref = refs[n_chunks]
    if first:
        out_ref, blocks = refs[n_chunks + 1:]
        rec_ref = None
    else:
        rec_ref, out_ref, blocks = refs[n_chunks + 1:]
    steps, batch, _ = chunk_refs[0].shape
    side = w_ref.shape[-1]
    rows = steps * batch
    for c in range(n_chunks):
        for i in range(local_blocks):
            x = chunk_refs[c][:, :, i * side:(i + 1) * side].astype(jnp.float32)
            blocks[c * local_blocks + i] = x.reshape(rows, side).astype(jnp.bfloat16)
    for j in range(local_blocks):
        if first:
            acc = jnp.zeros((rows, side), jnp.float32)
        else:
            acc = rec_ref[:, :, j * side:(j + 1) * side].reshape(rows, side)
        for k in range(nnz):
            x = blocks[pos_ref[j * nnz + k]]
            acc = acc + jnp.dot(x, w_ref[j, k], preferred_element_type=jnp.float32)
        out_ref[:, :, j * side:(j + 1) * side] = acc.reshape(steps, batch, side)


def round_contrib(pos, chunks, weights, rnd, rec):
    steps, batch, local = chunks[0].shape
    rounds, _, local_blocks, nnz, side, _ = weights.shape
    n_chunks = len(chunks)
    first = rec is None
    chunk_spec = pl.BlockSpec((steps, batch, local), lambda g, p: (0, 0, 0))
    w_spec = pl.BlockSpec(
        (None, None, local_blocks, nnz, side, side), lambda g, p: (rnd, 0, 0, 0, 0, 0)
    )
    rec_spec = pl.BlockSpec((steps, batch, local), lambda g, p: (0, 0, 0))
    in_specs = [chunk_spec] * n_chunks + [w_spec] + ([] if first else [rec_spec])
    operands = list(chunks) + [weights] + ([] if first else [rec])
    kernel = functools.partial(
        round_kernel, n_chunks=n_chunks, local_blocks=local_blocks, nnz=nnz, first=first
    )
    return pl.pallas_call(
        kernel,
        grid_spec=pltpu.PrefetchScalarGridSpec(
            num_scalar_prefetch=1,
            grid=(1,),
            in_specs=in_specs,
            out_specs=rec_spec,
            scratch_shapes=[pltpu.VMEM((n_chunks * local_blocks, steps * batch, side), jnp.bfloat16)],
        ),
        out_shape=jax.ShapeDtypeStruct((steps, batch, local), jnp.float32),
        input_output_aliases={} if first else {1 + n_chunks + 1: 0},
    )(pos, *operands)


def adjoint_scan(err_grad, surrogate, rec, lv_end, la_end, alpha, rho, beta):
    steps = err_grad.shape[0]
    lv_now, la_now = lv_end, la_end
    currents = [None] * steps
    for t in reversed(range(steps)):
        total = err_grad[t] + rec[t] - lv_now + la_now
        currents[t] = lv_now.astype(jnp.bfloat16)
        lv_next = alpha * lv_now + surrogate[t] * total
        la_next = rho * la_now - beta * surrogate[t] * total
        lv_now, la_now = lv_next, la_next
    return (jnp.stack(currents), lv_now, la_now)


def per_device(
    window, err_grad, surrogate, lv_end, la_end, alpha, rho, beta, weights, block_index, delays
):
    steps = err_grad.shape[0]
    local_neurons = err_grad.shape[2]
    block_side = weights.shape[-1]
    local_blocks = local_neurons // block_side
    rounds = weights.shape[0]
    levels = lax.axis_size("area").bit_length() - 1
    nbits = lax.axis_size("neuron").bit_length() - 1
    me_area = lax.axis_index("area")
    me_neuron = lax.axis_index("neuron")
    uses = {}
    for rnd in range(rounds):
        uses.setdefault(rnd % levels, []).append(rnd)
    whole = {}
    for bit, rnds in uses.items():
        if len(rnds) > 1:
            whole[bit] = swap(window, "area", 1 << bit)
    rec = None
    for rnd in range(rounds):
        bit = rnd % levels
        mask = 1 << bit
        if bit in whole:
            start = delays[rnd, me_area] - steps
            arrived = lax.dynamic_slice_in_dim(whole[bit], start, steps, 0)
        else:
            start = delays[rnd, me_area ^ mask] - steps
            piece = lax.dynamic_slice_in_dim(window, start, steps, 0)
            arrived = swap(piece, "area", mask)
        chunks = gather_neuron(arrived)
        idx = block_index[rnd, 0]
        owner = idx // local_blocks
        pos = relative_position(owner, me_neuron, nbits) * local_blocks + idx % local_blocks
        rec = round_contrib(pos.reshape(-1).astype(jnp.int32), chunks, weights, rnd, rec)
    return adjoint_scan(err_grad, surrogate, rec, lv_end, la_end, alpha, rho, beta)


def solution(mesh):
    placed = (
        P(None, "groups", ("area", "neuron")),
        P(None, "groups", ("area", "neuron")),
        P(None, "groups", ("area", "neuron")),
        P("groups", ("area", "neuron")),
        P("groups", ("area", "neuron")),
        P(("area", "neuron")),
        P(("area", "neuron")),
        P(("area", "neuron")),
        P(None, "area", "neuron", None, None, None),
        P(None, "area", "neuron", None),
        P(),
    )
    return jax.shard_map(
        per_device,
        mesh=mesh,
        in_specs=placed,
        out_specs=(
            P(None, "groups", ("area", "neuron")),
            P("groups", ("area", "neuron")),
            P("groups", ("area", "neuron")),
        ),
        check_vma=False,
    )
```

```python
import functools

import jax
import jax.numpy as jnp
from jax import lax
from jax.experimental import pallas as pl
from jax.experimental.pallas import tpu as pltpu
from jax.sharding import PartitionSpec as P


def swap(value, axis, mask):
    pairs = [(source, source ^ mask) for source in range(lax.axis_size(axis))]
    return lax.ppermute(value, axis, pairs)


def gather_neuron(piece):
    size = lax.axis_size("neuron")
    bits = size.bit_length() - 1
    held = [piece]
    for bit in reversed(range(bits)):
        held = held + [swap(chunk, "neuron", 1 << bit) for chunk in held]
    return held


def relative_position(n, me, bits):
    d = n ^ me
    pos = jnp.zeros_like(d)
    for s, bit in enumerate(reversed(range(bits))):
        pos = pos | (((d >> bit) & 1) << s)
    return pos


def round_kernel(pos_ref, *refs, n_chunks, local_blocks, nnz, mode):
    chunk_refs = refs[:n_chunks]
    w_ref = refs[n_chunks]
    rest = refs[n_chunks + 1:]
    if mode == "first":
        (out_ref, blocks) = rest
    elif mode == "middle":
        (rec_ref, out_ref, blocks) = rest
    else:
        (rec_ref, err_ref, surr_ref, lv_ref, la_ref, alpha_ref, rho_ref, beta_ref,
         cur_ref, lv_out, la_out, blocks) = rest
    steps, batch, _ = chunk_refs[0].shape
    side = w_ref.shape[-1]
    rows = steps * batch
    for c in range(n_chunks):
        for i in range(local_blocks):
            x = chunk_refs[c][:, :, i * side:(i + 1) * side].astype(jnp.float32)
            blocks[c * local_blocks + i] = x.reshape(rows, side).astype(jnp.bfloat16)
    for j in range(local_blocks):
        cols = slice(j * side, (j + 1) * side)
        if mode == "first":
            acc = jnp.zeros((rows, side), jnp.float32)
        else:
            acc = rec_ref[:, :, cols].reshape(rows, side)
        for k in range(nnz):
            x = blocks[pos_ref[j * nnz + k]]
            acc = acc + jnp.dot(x, w_ref[j, k], preferred_element_type=jnp.float32)
        rec = acc.reshape(steps, batch, side)
        if mode != "final":
            out_ref[:, :, cols] = rec
            continue
        alpha = alpha_ref[:, cols]
        rho = rho_ref[:, cols]
        beta = beta_ref[:, cols]
        lv_now = lv_ref[:, cols]
        la_now = la_ref[:, cols]
        for t in reversed(range(steps)):
            surr = surr_ref[t, :, cols]
            total = err_ref[t, :, cols] + rec[t] - lv_now + la_now
            cur_ref[t, :, cols] = lv_now.astype(cur_ref.dtype)
            lv_next = alpha * lv_now + surr * total
            la_next = rho * la_now - beta * surr * total
            lv_now, la_now = lv_next, la_next
        lv_out[:, cols] = lv_now
        la_out[:, cols] = la_now


def round_contrib(pos, chunks, weights, rnd, rec, scan_args=None):
    steps, batch, local = chunks[0].shape
    rounds, _, local_blocks, nnz, side, _ = weights.shape
    n_chunks = len(chunks)
    mode = "first" if rec is None else ("middle" if scan_args is None else "final")
    full3 = pl.BlockSpec((steps, batch, local), lambda g, p: (0, 0, 0))
    full2 = pl.BlockSpec((batch, local), lambda g, p: (0, 0))
    row = pl.BlockSpec((1, local), lambda g, p: (0, 0))
    w_spec = pl.BlockSpec(
        (None, None, local_blocks, nnz, side, side), lambda g, p: (rnd, 0, 0, 0, 0, 0)
    )
    in_specs = [full3] * n_chunks + [w_spec]
    operands = list(chunks) + [weights]
    aliases = {}
    if mode != "first":
        in_specs.append(full3)
        operands.append(rec)
    if mode == "middle":
        aliases = {1 + n_chunks + 1: 0}
    if mode == "final":
        err_grad, surrogate, lv_end, la_end, alpha, rho, beta = scan_args
        in_specs += [full3, full3, full2, full2, row, row, row]
        operands += [err_grad, surrogate, lv_end, la_end,
                     alpha.reshape(1, local), rho.reshape(1, local), beta.reshape(1, local)]
        out_specs = (full3, full2, full2)
        out_shape = (
            jax.ShapeDtypeStruct((steps, batch, local), jnp.bfloat16),
            jax.ShapeDtypeStruct((batch, local), jnp.float32),
            jax.ShapeDtypeStruct((batch, local), jnp.float32),
        )
    else:
        out_specs = full3
        out_shape = jax.ShapeDtypeStruct((steps, batch, local), jnp.float32)
    kernel = functools.partial(
        round_kernel, n_chunks=n_chunks, local_blocks=local_blocks, nnz=nnz, mode=mode
    )
    return pl.pallas_call(
        kernel,
        grid_spec=pltpu.PrefetchScalarGridSpec(
            num_scalar_prefetch=1,
            grid=(1,),
            in_specs=in_specs,
            out_specs=out_specs,
            scratch_shapes=[pltpu.VMEM((n_chunks * local_blocks, steps * batch, side), jnp.bfloat16)],
        ),
        out_shape=out_shape,
        input_output_aliases=aliases,
    )(pos, *operands)


def per_device(
    window, err_grad, surrogate, lv_end, la_end, alpha, rho, beta, weights, block_index, delays
):
    steps = err_grad.shape[0]
    local_neurons = err_grad.shape[2]
    block_side = weights.shape[-1]
    local_blocks = local_neurons // block_side
    rounds = weights.shape[0]
    levels = lax.axis_size("area").bit_length() - 1
    nbits = lax.axis_size("neuron").bit_length() - 1
    me_area = lax.axis_index("area")
    me_neuron = lax.axis_index("neuron")
    arrived = []
    gate = None
    for first in range(0, rounds, 2):
        stage = list(range(first, min(first + 2, rounds)))
        pieces = []
        for rnd in stage:
            mask = 1 << (rnd % levels)
            start = delays[rnd, me_area ^ mask] - steps
            pieces.append(lax.dynamic_slice_in_dim(window, start, steps, 0))
        if gate is not None:
            pieces, _ = lax.optimization_barrier((pieces, gate))
        got = [swap(piece, "area", 1 << (rnd % levels)) for piece, rnd in zip(pieces, stage)]
        arrived += got
        gate = got
    rec = None
    for rnd in range(rounds):
        chunks = gather_neuron(arrived[rnd])
        idx = block_index[rnd, 0]
        owner = idx // local_blocks
        pos = relative_position(owner, me_neuron, nbits) * local_blocks + idx % local_blocks
        scan_args = None
        if rnd == rounds - 1:
            scan_args = (err_grad, surrogate, lv_end, la_end, alpha, rho, beta)
        rec = round_contrib(pos.reshape(-1).astype(jnp.int32), chunks, weights, rnd, rec, scan_args)
    return rec


def solution(mesh):
    placed = (
        P(None, "groups", ("area", "neuron")),
        P(None, "groups", ("area", "neuron")),
        P(None, "groups", ("area", "neuron")),
        P("groups", ("area", "neuron")),
        P("groups", ("area", "neuron")),
        P(("area", "neuron")),
        P(("area", "neuron")),
        P(("area", "neuron")),
        P(None, "area", "neuron", None, None, None),
        P(None, "area", "neuron", None),
        P(),
    )
    return jax.shard_map(
        per_device,
        mesh=mesh,
        in_specs=placed,
        out_specs=(
            P(None, "groups", ("area", "neuron")),
            P("groups", ("area", "neuron")),
            P("groups", ("area", "neuron")),
        ),
        check_vma=False,
    )
```

```python
import functools

import jax
import jax.numpy as jnp
from jax import lax
from jax.experimental import pallas as pl
from jax.experimental.pallas import tpu as pltpu
from jax.sharding import PartitionSpec as P


def swap(value, axis, mask):
    pairs = [(source, source ^ mask) for source in range(lax.axis_size(axis))]
    return lax.ppermute(value, axis, pairs)


def gather_neuron(piece):
    size = lax.axis_size("neuron")
    bits = size.bit_length() - 1
    held = [piece]
    for bit in reversed(range(bits)):
        held = held + [swap(chunk, "neuron", 1 << bit) for chunk in held]
    return held


def relative_position(n, me, bits):
    d = n ^ me
    pos = jnp.zeros_like(d)
    for s, bit in enumerate(reversed(range(bits))):
        pos = pos | (((d >> bit) & 1) << s)
    return pos


def round_kernel(pos_ref, *refs, n_chunks, n_halves, local_blocks, nnz, mode):
    n_in = n_chunks * n_halves
    chunk_refs = refs[:n_in]
    w_ref = refs[n_in]
    rest = refs[n_in + 1:]
    if mode == "first":
        (out_ref, blocks) = rest
    elif mode == "middle":
        (rec_ref, out_ref, blocks) = rest
    else:
        (rec_ref, err_ref, surr_ref, lv_ref, la_ref, alpha_ref, rho_ref, beta_ref,
         cur_ref, lv_out, la_out, blocks) = rest
    steps, batch, _ = chunk_refs[0].shape
    side = w_ref.shape[-1]
    rows = steps * batch
    per_half = local_blocks // n_halves
    for c in range(n_chunks):
        for i in range(local_blocks):
            src = chunk_refs[c * n_halves + i // per_half]
            off = (i % per_half) * side
            x = src[:, :, off:off + side].astype(jnp.float32)
            blocks[c * local_blocks + i] = x.reshape(rows, side).astype(jnp.bfloat16)
    for j in range(local_blocks):
        cols = slice(j * side, (j + 1) * side)
        if mode == "first":
            acc = jnp.zeros((rows, side), jnp.float32)
        else:
            acc = rec_ref[:, :, cols].reshape(rows, side)
        for k in range(nnz):
            x = blocks[pos_ref[j * nnz + k]]
            acc = acc + jnp.dot(x, w_ref[j, k], preferred_element_type=jnp.float32)
        rec = acc.reshape(steps, batch, side)
        if mode != "final":
            out_ref[:, :, cols] = rec
            continue
        alpha = alpha_ref[:, cols]
        rho = rho_ref[:, cols]
        beta = beta_ref[:, cols]
        lv_now = lv_ref[:, cols]
        la_now = la_ref[:, cols]
        for t in reversed(range(steps)):
            surr = surr_ref[t, :, cols]
            total = err_ref[t, :, cols] + rec[t] - lv_now + la_now
            cur_ref[t, :, cols] = lv_now.astype(cur_ref.dtype)
            lv_next = alpha * lv_now + surr * total
            la_next = rho * la_now - beta * surr * total
            lv_now, la_now = lv_next, la_next
        lv_out[:, cols] = lv_now
        la_out[:, cols] = la_now


def round_contrib(pos, chunks, n_halves, w_round, rec, scan_args=None):
    steps, batch, _ = chunks[0].shape
    local_blocks, nnz, side, _ = w_round.shape
    local = local_blocks * side
    n_chunks = len(chunks) // n_halves
    mode = "first" if rec is None else ("middle" if scan_args is None else "final")
    vmem = pl.BlockSpec(memory_space=pltpu.VMEM)
    operands = list(chunks) + [w_round]
    if mode != "first":
        operands.append(rec)
    aliases = {}
    if mode == "middle":
        aliases = {len(operands): 0}
    if mode == "final":
        err_grad, surrogate, lv_end, la_end, alpha, rho, beta = scan_args
        operands += [err_grad, surrogate, lv_end, la_end,
                     alpha.reshape(1, local), rho.reshape(1, local), beta.reshape(1, local)]
        out_specs = (vmem, vmem, vmem)
        out_shape = (
            jax.ShapeDtypeStruct((steps, batch, local), jnp.bfloat16),
            jax.ShapeDtypeStruct((batch, local), jnp.float32),
            jax.ShapeDtypeStruct((batch, local), jnp.float32),
        )
    else:
        out_specs = vmem
        out_shape = jax.ShapeDtypeStruct((steps, batch, local), jnp.float32)
    kernel = functools.partial(
        round_kernel, n_chunks=n_chunks, n_halves=n_halves, local_blocks=local_blocks,
        nnz=nnz, mode=mode,
    )
    return pl.pallas_call(
        kernel,
        in_specs=[pl.BlockSpec(memory_space=pltpu.SMEM)] + [vmem] * len(operands),
        out_specs=out_specs,
        scratch_shapes=[pltpu.VMEM((n_chunks * local_blocks, steps * batch, side), jnp.bfloat16)],
        out_shape=out_shape,
        input_output_aliases=aliases,
    )(pos, *operands)


def per_device(
    window, err_grad, surrogate, lv_end, la_end, alpha, rho, beta, weights, block_index, delays
):
    steps = err_grad.shape[0]
    local_neurons = err_grad.shape[2]
    block_side = weights.shape[-1]
    local_blocks = local_neurons // block_side
    rounds = weights.shape[0]
    levels = lax.axis_size("area").bit_length() - 1
    nbits = lax.axis_size("neuron").bit_length() - 1
    me_area = lax.axis_index("area")
    me_neuron = lax.axis_index("neuron")
    n_halves = 2 if local_blocks % 2 == 0 else 1
    width = local_neurons // n_halves
    arrived = {}
    gate = None
    for first in range(0, rounds, 2):
        pair = list(range(first, min(first + 2, rounds)))
        for h in range(n_halves):
            pieces = []
            for rnd in pair:
                mask = 1 << (rnd % levels)
                start = delays[rnd, me_area ^ mask] - steps
                piece = lax.dynamic_slice_in_dim(window, start, steps, 0)
                pieces.append(piece[:, :, h * width:(h + 1) * width])
            if gate is not None:
                pieces, _ = lax.optimization_barrier((pieces, gate))
            got = [swap(piece, "area", 1 << (rnd % levels)) for piece, rnd in zip(pieces, pair)]
            for rnd, g in zip(pair, got):
                arrived[(rnd, h)] = g
            gate = got
    rec = None
    for rnd in range(rounds):
        halves = [gather_neuron(arrived[(rnd, h)]) for h in range(n_halves)]
        chunks = [halves[h][c] for c in range(len(halves[0])) for h in range(n_halves)]
        idx = block_index[rnd, 0]
        owner = idx // local_blocks
        pos = relative_position(owner, me_neuron, nbits) * local_blocks + idx % local_blocks
        scan_args = None
        if rnd == rounds - 1:
            scan_args = (err_grad, surrogate, lv_end, la_end, alpha, rho, beta)
        rec = round_contrib(
            pos.reshape(-1).astype(jnp.int32), chunks, n_halves, weights[rnd, 0], rec, scan_args
        )
    return rec


def solution(mesh):
    placed = (
        P(None, "groups", ("area", "neuron")),
        P(None, "groups", ("area", "neuron")),
        P(None, "groups", ("area", "neuron")),
        P("groups", ("area", "neuron")),
        P("groups", ("area", "neuron")),
        P(("area", "neuron")),
        P(("area", "neuron")),
        P(("area", "neuron")),
        P(None, "area", "neuron", None, None, None),
        P(None, "area", "neuron", None),
        P(),
    )
    return jax.shard_map(
        per_device,
        mesh=mesh,
        in_specs=placed,
        out_specs=(
            P(None, "groups", ("area", "neuron")),
            P("groups", ("area", "neuron")),
            P("groups", ("area", "neuron")),
        ),
        check_vma=False,
    )
```

```python
import functools

import jax
import jax.numpy as jnp
from jax import lax
from jax.experimental import pallas as pl
from jax.experimental.pallas import tpu as pltpu
from jax.sharding import PartitionSpec as P

ANY = pl.BlockSpec(memory_space=pl.ANY)
SMEM = pl.BlockSpec(memory_space=pltpu.SMEM)
VMEM = pl.BlockSpec(memory_space=pltpu.VMEM)


def swap(value, axis, mask):
    pairs = [(source, source ^ mask) for source in range(lax.axis_size(axis))]
    return lax.ppermute(value, axis, pairs)


def slice_kernel(delays_ref, window_ref, *refs, rounds, levels, steps):
    outs = refs[:rounds]
    sem = refs[rounds]
    me = lax.axis_index("area")
    copies = []
    for rnd in range(rounds):
        start = delays_ref[rnd, me ^ (1 << (rnd % levels))] - steps
        copy = pltpu.make_async_copy(window_ref.at[pl.ds(start, steps)], outs[rnd], sem.at[rnd])
        copy.start()
        copies.append(copy)
    for copy in copies:
        copy.wait()


def send_slices(window, delays, rounds, levels, steps):
    shape = (steps,) + window.shape[1:]
    kernel = functools.partial(slice_kernel, rounds=rounds, levels=levels, steps=steps)
    return pl.pallas_call(
        kernel,
        in_specs=[SMEM, ANY],
        out_specs=[ANY] * rounds,
        out_shape=[jax.ShapeDtypeStruct(shape, window.dtype)] * rounds,
        scratch_shapes=[pltpu.SemaphoreType.DMA((rounds,))],
    )(delays, window)


def gather_neuron(stacked):
    bits = lax.axis_size("neuron").bit_length() - 1
    pieces = [stacked]
    for bit in reversed(range(bits)):
        sent = pieces[0] if len(pieces) == 1 else jnp.concatenate(pieces, axis=0)
        pieces.append(swap(sent, "neuron", 1 << bit))
    return pieces


def chunk_place(p, ri, n_rounds):
    if p == 0:
        return 0, ri
    k = p.bit_length()
    return k, (p - (1 << (k - 1))) * n_rounds + ri


def relative_position(n, me, bits):
    d = n ^ me
    pos = jnp.zeros_like(d)
    for s, bit in enumerate(reversed(range(bits))):
        pos = pos | (((d >> bit) & 1) << s)
    return pos


def stage_kernel(pos_ref, *refs, n_pieces, stage, n_pos, final, has_rec):
    n_rounds = len(stage)
    it = iter(refs)
    piece_hbm = [next(it) for _ in range(n_pieces)]
    w_hbm = next(it)
    rec_hbm = next(it) if has_rec else None
    if final:
        err_hbm, surr_hbm, lv_hbm, la_hbm, alpha_hbm, rho_hbm, beta_hbm = [next(it) for _ in range(7)]
        cur_ref, lv_out, la_out = next(it), next(it), next(it)
    else:
        out_ref = next(it)
    piece_buf = [next(it) for _ in range(n_pieces)]
    w_buf = next(it)
    blocks = next(it)
    sem = next(it)
    if has_rec:
        rec_buf = next(it)
    if final:
        err_buf, surr_buf, lv_buf, la_buf, alpha_buf, rho_buf, beta_buf = [next(it) for _ in range(7)]

    _, steps, batch, width = piece_hbm[0].shape
    local_blocks, nnz, side = w_buf.shape[1], w_buf.shape[2], w_buf.shape[3]
    rows = steps * batch
    n_sem = 0

    def start(src, dst):
        nonlocal n_sem
        copy = pltpu.make_async_copy(src, dst, sem.at[n_sem])
        n_sem += 1
        copy.start()
        return copy

    piece_cp = [start(piece_hbm[k], piece_buf[k]) for k in range(n_pieces)]
    w_cp = [start(w_hbm.at[rnd, 0], w_buf.at[ri]) for ri, rnd in enumerate(stage)]
    rec_cp = start(rec_hbm, rec_buf) if has_rec else None
    if final:
        scan_cp = [
            start(src, dst)
            for src, dst in zip(
                (err_hbm, surr_hbm, lv_hbm, la_hbm, alpha_hbm, rho_hbm, beta_hbm),
                (err_buf, surr_buf, lv_buf, la_buf, alpha_buf, rho_buf, beta_buf),
            )
        ]

    waited = set()
    for ri in range(n_rounds):
        for p in range(n_pos):
            k, e = chunk_place(p, ri, n_rounds)
            if k not in waited:
                piece_cp[k].wait()
                waited.add(k)
            for i in range(local_blocks):
                x = piece_buf[k][e, :, :, i * side:(i + 1) * side].astype(jnp.float32)
                blocks[(ri * n_pos + p) * local_blocks + i] = x.reshape(rows, side).astype(jnp.bfloat16)
    if has_rec:
        rec_cp.wait()
    for ri in range(n_rounds):
        w_cp[ri].wait()
    if final:
        for copy in scan_cp:
            copy.wait()
    for j in range(local_blocks):
        cols = slice(j * side, (j + 1) * side)
        if has_rec:
            acc = rec_buf[:, :, cols].reshape(rows, side)
        else:
            acc = jnp.zeros((rows, side), jnp.float32)
        for ri in range(n_rounds):
            for k in range(nnz):
                x = blocks[ri * n_pos * local_blocks + pos_ref[(ri * local_blocks + j) * nnz + k]]
                acc = acc + jnp.dot(x, w_buf[ri, j, k], preferred_element_type=jnp.float32)
        rec = acc.reshape(steps, batch, side)
        if not final:
            out_ref[:, :, cols] = rec
            continue
        alpha = alpha_buf[:, cols]
        rho = rho_buf[:, cols]
        beta = beta_buf[:, cols]
        lv_now = lv_buf[:, cols]
        la_now = la_buf[:, cols]
        for t in reversed(range(steps)):
            surr = surr_buf[t, :, cols]
            total = err_buf[t, :, cols] + rec[t] - lv_now + la_now
            cur_ref[t, :, cols] = lv_now.astype(cur_ref.dtype)
            lv_next = alpha * lv_now + surr * total
            la_next = rho * la_now - beta * surr * total
            lv_now, la_now = lv_next, la_next
        lv_out[:, cols] = lv_now
        la_out[:, cols] = la_now


def stage_contrib(pos, pieces, weights, stage, n_pos, rec, scan_args):
    _, steps, batch, local = pieces[0].shape
    _, _, local_blocks, nnz, side, _ = weights.shape
    n_rounds = len(stage)
    final = scan_args is not None
    has_rec = rec is not None
    operands = list(pieces) + [weights]
    scratch = [pltpu.VMEM(p.shape, p.dtype) for p in pieces]
    scratch += [
        pltpu.VMEM((n_rounds, local_blocks, nnz, side, side), weights.dtype),
        pltpu.VMEM((n_rounds * n_pos * local_blocks, steps * batch, side), jnp.bfloat16),
    ]
    n_sem = len(pieces) + n_rounds + (1 if has_rec else 0) + (7 if final else 0)
    scratch.append(pltpu.SemaphoreType.DMA((n_sem,)))
    if has_rec:
        operands.append(rec)
        scratch.append(pltpu.VMEM(rec.shape, rec.dtype))
    if final:
        err_grad, surrogate, lv_end, la_end, alpha, rho, beta = scan_args
        rows = [a.reshape(1, local) for a in (alpha, rho, beta)]
        extra = [err_grad, surrogate, lv_end, la_end] + rows
        operands += extra
        scratch += [pltpu.VMEM(a.shape, a.dtype) for a in extra]
        out_specs = (VMEM, VMEM, VMEM)
        out_shape = (
            jax.ShapeDtypeStruct((steps, batch, local), jnp.bfloat16),
            jax.ShapeDtypeStruct((batch, local), jnp.float32),
            jax.ShapeDtypeStruct((batch, local), jnp.float32),
        )
    else:
        out_specs = VMEM
        out_shape = jax.ShapeDtypeStruct((steps, batch, local), jnp.float32)
    kernel = functools.partial(
        stage_kernel, n_pieces=len(pieces), stage=tuple(stage), n_pos=n_pos,
        final=final, has_rec=has_rec,
    )
    return pl.pallas_call(
        kernel,
        in_specs=[SMEM] + [ANY] * len(operands),
        out_specs=out_specs,
        scratch_shapes=scratch,
        out_shape=out_shape,
    )(pos, *operands)


def per_device(
    window, err_grad, surrogate, lv_end, la_end, alpha, rho, beta, weights, block_index, delays
):
    steps = err_grad.shape[0]
    local_neurons = err_grad.shape[2]
    block_side = weights.shape[-1]
    local_blocks = local_neurons // block_side
    rounds = weights.shape[0]
    levels = lax.axis_size("area").bit_length() - 1
    nbits = lax.axis_size("neuron").bit_length() - 1
    n_pos = 1 << nbits
    me_neuron = lax.axis_index("neuron")
    slices = send_slices(window, delays, rounds, levels, steps)
    stages = [list(range(f, min(f + 2, rounds))) for f in range(0, rounds, 2)]
    arrived = []
    gate = None
    for stage in stages:
        pieces = [slices[rnd] for rnd in stage]
        if gate is not None:
            pieces, _ = lax.optimization_barrier((pieces, gate))
        got = [swap(piece, "area", 1 << (rnd % levels)) for piece, rnd in zip(pieces, stage)]
        arrived.append(jnp.stack(got))
        gate = got
    rec = None
    for si, stage in enumerate(stages):
        stacked = arrived[si]
        if rec is not None:
            stacked, _ = lax.optimization_barrier((stacked, rec))
        pieces = gather_neuron(stacked)
        idx = block_index[jnp.array(stage), 0]
        owner = idx // local_blocks
        pos = relative_position(owner, me_neuron, nbits) * local_blocks + idx % local_blocks
        scan_args = None
        if si == len(stages) - 1:
            scan_args = (err_grad, surrogate, lv_end, la_end, alpha, rho, beta)
        rec = stage_contrib(
            pos.reshape(-1).astype(jnp.int32), pieces, weights, stage, n_pos, rec, scan_args
        )
    return rec


def solution(mesh):
    placed = (
        P(None, "groups", ("area", "neuron")),
        P(None, "groups", ("area", "neuron")),
        P(None, "groups", ("area", "neuron")),
        P("groups", ("area", "neuron")),
        P("groups", ("area", "neuron")),
        P(("area", "neuron")),
        P(("area", "neuron")),
        P(("area", "neuron")),
        P(None, "area", "neuron", None, None, None),
        P(None, "area", "neuron", None),
        P(),
    )
    return jax.shard_map(
        per_device,
        mesh=mesh,
        in_specs=placed,
        out_specs=(
            P(None, "groups", ("area", "neuron")),
            P("groups", ("area", "neuron")),
            P("groups", ("area", "neuron")),
        ),
        check_vma=False,
    )
```

```python
import functools

import jax
import jax.numpy as jnp
from jax import lax
from jax.experimental import pallas as pl
from jax.experimental.pallas import tpu as pltpu
from jax.sharding import PartitionSpec as P

ANY = pl.BlockSpec(memory_space=pl.ANY)
SMEM = pl.BlockSpec(memory_space=pltpu.SMEM)
VMEM = pl.BlockSpec(memory_space=pltpu.VMEM)


def swap(value, axis, mask):
    pairs = [(source, source ^ mask) for source in range(lax.axis_size(axis))]
    return lax.ppermute(value, axis, pairs)


def slice_kernel(delays_ref, window_ref, *outs, levels, steps):
    me = lax.axis_index("area")
    for rnd, out in enumerate(outs):
        start = delays_ref[rnd, me ^ (1 << (rnd % levels))] - steps
        out[...] = window_ref[pl.ds(start, steps)]


def send_slices(window, delays, rounds, levels, steps):
    shape = (steps,) + window.shape[1:]
    kernel = functools.partial(slice_kernel, levels=levels, steps=steps)
    return pl.pallas_call(
        kernel,
        in_specs=[SMEM, VMEM],
        out_specs=[VMEM] * rounds,
        out_shape=[jax.ShapeDtypeStruct(shape, window.dtype)] * rounds,
    )(delays, window)


def gather_neuron(piece, gate=None):
    bits = lax.axis_size("neuron").bit_length() - 1
    held = [piece]
    for bit in reversed(range(bits)):
        if bit == 0 and gate is not None:
            held, _ = lax.optimization_barrier((held, gate))
        held = held + [swap(chunk, "neuron", 1 << bit) for chunk in held]
    return held


def relative_position(n, me, bits):
    d = n ^ me
    pos = jnp.zeros_like(d)
    for s, bit in enumerate(reversed(range(bits))):
        pos = pos | (((d >> bit) & 1) << s)
    return pos


def stage_kernel(pos_ref, *refs, n_pieces, stage, n_pos, final, has_rec):
    n_rounds = len(stage)
    it = iter(refs)
    piece_hbm = [next(it) for _ in range(n_pieces)]
    w_hbm = next(it)
    rec_hbm = next(it) if has_rec else None
    if final:
        err_hbm, surr_hbm, lv_hbm, la_hbm, alpha_hbm, rho_hbm, beta_hbm = [next(it) for _ in range(7)]
        cur_ref, lv_out, la_out = next(it), next(it), next(it)
    else:
        out_ref = next(it)
    piece_buf = [next(it) for _ in range(n_pieces)]
    w_buf = next(it)
    blocks = next(it)
    sem = next(it)
    if has_rec:
        rec_buf = next(it)
    if final:
        err_buf, surr_buf, lv_buf, la_buf, alpha_buf, rho_buf, beta_buf = [next(it) for _ in range(7)]

    steps, batch, width = piece_hbm[0].shape
    local_blocks, nnz, side = w_buf.shape[1], w_buf.shape[2], w_buf.shape[3]
    rows = steps * batch
    n_sem = 0

    def start(src, dst):
        nonlocal n_sem
        copy = pltpu.make_async_copy(src, dst, sem.at[n_sem])
        n_sem += 1
        copy.start()
        return copy

    piece_cp = [start(piece_hbm[k], piece_buf[k]) for k in range(n_pieces)]
    w_cp = [start(w_hbm.at[rnd, 0], w_buf.at[ri]) for ri, rnd in enumerate(stage)]
    rec_cp = start(rec_hbm, rec_buf) if has_rec else None
    if final:
        scan_cp = [
            start(src, dst)
            for src, dst in zip(
                (err_hbm, surr_hbm, lv_hbm, la_hbm, alpha_hbm, rho_hbm, beta_hbm),
                (err_buf, surr_buf, lv_buf, la_buf, alpha_buf, rho_buf, beta_buf),
            )
        ]

    for ri in range(n_rounds):
        for p in range(n_pos):
            k = ri * n_pos + p
            piece_cp[k].wait()
            for i in range(local_blocks):
                x = piece_buf[k][:, :, i * side:(i + 1) * side].astype(jnp.float32)
                blocks[(ri * n_pos + p) * local_blocks + i] = x.reshape(rows, side).astype(jnp.bfloat16)
    if has_rec:
        rec_cp.wait()
    for ri in range(n_rounds):
        w_cp[ri].wait()
    if final:
        for copy in scan_cp:
            copy.wait()
    for j in range(local_blocks):
        cols = slice(j * side, (j + 1) * side)
        if has_rec:
            acc = rec_buf[:, :, cols].reshape(rows, side)
        else:
            acc = jnp.zeros((rows, side), jnp.float32)
        for ri in range(n_rounds):
            for k in range(nnz):
                x = blocks[ri * n_pos * local_blocks + pos_ref[(ri * local_blocks + j) * nnz + k]]
                acc = acc + jnp.dot(x, w_buf[ri, j, k], preferred_element_type=jnp.float32)
        rec = acc.reshape(steps, batch, side)
        if not final:
            out_ref[:, :, cols] = rec
            continue
        alpha = alpha_buf[:, cols]
        rho = rho_buf[:, cols]
        beta = beta_buf[:, cols]
        lv_now = lv_buf[:, cols]
        la_now = la_buf[:, cols]
        for t in reversed(range(steps)):
            surr = surr_buf[t, :, cols]
            total = err_buf[t, :, cols] + rec[t] - lv_now + la_now
            cur_ref[t, :, cols] = lv_now.astype(cur_ref.dtype)
            lv_next = alpha * lv_now + surr * total
            la_next = rho * la_now - beta * surr * total
            lv_now, la_now = lv_next, la_next
        lv_out[:, cols] = lv_now
        la_out[:, cols] = la_now


def stage_contrib(pos, pieces, weights, stage, n_pos, rec, scan_args):
    steps, batch, local = pieces[0].shape
    _, _, local_blocks, nnz, side, _ = weights.shape
    n_rounds = len(stage)
    final = scan_args is not None
    has_rec = rec is not None
    operands = list(pieces) + [weights]
    scratch = [pltpu.VMEM(p.shape, p.dtype) for p in pieces]
    scratch += [
        pltpu.VMEM((n_rounds, local_blocks, nnz, side, side), weights.dtype),
        pltpu.VMEM((n_rounds * n_pos * local_blocks, steps * batch, side), jnp.bfloat16),
    ]
    n_sem = len(pieces) + n_rounds + (1 if has_rec else 0) + (7 if final else 0)
    scratch.append(pltpu.SemaphoreType.DMA((n_sem,)))
    if has_rec:
        operands.append(rec)
        scratch.append(pltpu.VMEM(rec.shape, rec.dtype))
    if final:
        err_grad, surrogate, lv_end, la_end, alpha, rho, beta = scan_args
        rows = [a.reshape(1, local) for a in (alpha, rho, beta)]
        extra = [err_grad, surrogate, lv_end, la_end] + rows
        operands += extra
        scratch += [pltpu.VMEM(a.shape, a.dtype) for a in extra]
        out_specs = (VMEM, VMEM, VMEM)
        out_shape = (
            jax.ShapeDtypeStruct((steps, batch, local), jnp.bfloat16),
            jax.ShapeDtypeStruct((batch, local), jnp.float32),
            jax.ShapeDtypeStruct((batch, local), jnp.float32),
        )
    else:
        out_specs = VMEM
        out_shape = jax.ShapeDtypeStruct((steps, batch, local), jnp.float32)
    kernel = functools.partial(
        stage_kernel, n_pieces=len(pieces), stage=tuple(stage), n_pos=n_pos,
        final=final, has_rec=has_rec,
    )
    return pl.pallas_call(
        kernel,
        in_specs=[SMEM] + [ANY] * len(operands),
        out_specs=out_specs,
        scratch_shapes=scratch,
        out_shape=out_shape,
    )(pos, *operands)


def per_device(
    window, err_grad, surrogate, lv_end, la_end, alpha, rho, beta, weights, block_index, delays
):
    steps = err_grad.shape[0]
    local_neurons = err_grad.shape[2]
    block_side = weights.shape[-1]
    local_blocks = local_neurons // block_side
    rounds = weights.shape[0]
    levels = lax.axis_size("area").bit_length() - 1
    nbits = lax.axis_size("neuron").bit_length() - 1
    n_pos = 1 << nbits
    me_neuron = lax.axis_index("neuron")
    slices = send_slices(window, delays, rounds, levels, steps)
    stages = [list(range(f, min(f + 2, rounds))) for f in range(0, rounds, 2)]
    arrived = []
    gate = None
    for stage in stages:
        pieces = [slices[rnd] for rnd in stage]
        if gate is not None:
            pieces, _ = lax.optimization_barrier((pieces, gate))
        got = [swap(piece, "area", 1 << (rnd % levels)) for piece, rnd in zip(pieces, stage)]
        arrived += got
        gate = got
    rec = None
    for si, stage in enumerate(stages):
        chunks = []
        for rnd in stage:
            chunks += gather_neuron(arrived[rnd], rec)
        idx = block_index[jnp.array(stage), 0]
        owner = idx // local_blocks
        pos = relative_position(owner, me_neuron, nbits) * local_blocks + idx % local_blocks
        scan_args = None
        if si == len(stages) - 1:
            scan_args = (err_grad, surrogate, lv_end, la_end, alpha, rho, beta)
        rec = stage_contrib(
            pos.reshape(-1).astype(jnp.int32), chunks, weights, stage, n_pos, rec, scan_args
        )
    return rec


def solution(mesh):
    placed = (
        P(None, "groups", ("area", "neuron")),
        P(None, "groups", ("area", "neuron")),
        P(None, "groups", ("area", "neuron")),
        P("groups", ("area", "neuron")),
        P("groups", ("area", "neuron")),
        P(("area", "neuron")),
        P(("area", "neuron")),
        P(("area", "neuron")),
        P(None, "area", "neuron", None, None, None),
        P(None, "area", "neuron", None),
        P(),
    )
    return jax.shard_map(
        per_device,
        mesh=mesh,
        in_specs=placed,
        out_specs=(
            P(None, "groups", ("area", "neuron")),
            P("groups", ("area", "neuron")),
            P("groups", ("area", "neuron")),
        ),
        check_vma=False,
    )
```

```python
import functools

import jax
import jax.numpy as jnp
from jax import lax
from jax.experimental import pallas as pl
from jax.experimental.pallas import tpu as pltpu
from jax.sharding import PartitionSpec as P

ANY = pl.BlockSpec(memory_space=pl.ANY)
SMEM = pl.BlockSpec(memory_space=pltpu.SMEM)
VMEM = pl.BlockSpec(memory_space=pltpu.VMEM)


def swap(value, axis, mask):
    pairs = [(source, source ^ mask) for source in range(lax.axis_size(axis))]
    return lax.ppermute(value, axis, pairs)


def slice_kernel(delays_ref, window_ref, *outs, levels, steps):
    me = lax.axis_index("area")
    for rnd, out in enumerate(outs):
        start = delays_ref[rnd, me ^ (1 << (rnd % levels))] - steps
        out[...] = window_ref[pl.ds(start, steps)]


def send_slices(window, delays, rounds, levels, steps):
    shape = (steps,) + window.shape[1:]
    kernel = functools.partial(slice_kernel, levels=levels, steps=steps)
    return pl.pallas_call(
        kernel,
        in_specs=[SMEM, VMEM],
        out_specs=[VMEM] * rounds,
        out_shape=[jax.ShapeDtypeStruct(shape, window.dtype)] * rounds,
    )(delays, window)


def gather_neuron(piece, gate=None):
    bits = lax.axis_size("neuron").bit_length() - 1
    held = [piece]
    for bit in reversed(range(bits)):
        if bit == 0 and gate is not None:
            held, _ = lax.optimization_barrier((held, gate))
        held = held + [swap(chunk, "neuron", 1 << bit) for chunk in held]
    return held


def stage_kernel(bi_ref, *refs, n_pieces, stage, n_pos, final, has_rec):
    n_rounds = len(stage)
    it = iter(refs)
    piece_hbm = [next(it) for _ in range(n_pieces)]
    w_hbm = next(it)
    rec_hbm = next(it) if has_rec else None
    if final:
        scan_hbm = [next(it) for _ in range(7)]
        cur_ref, lv_out, la_out = next(it), next(it), next(it)
    else:
        out_ref = next(it)
    piece_buf = [next(it) for _ in range(n_pieces)]
    w_buf = next(it)
    blocks = next(it)
    sem = next(it)
    rec_buf = next(it)
    if final:
        scan_buf = [next(it) for _ in range(7)]

    steps, batch, width = piece_hbm[0].shape
    local_blocks, nnz, side = w_buf.shape[1], w_buf.shape[2], w_buf.shape[3]
    rows = steps * batch
    bits = n_pos.bit_length() - 1
    me = lax.axis_index("neuron")
    n_sem = 0

    def start(src, dst):
        nonlocal n_sem
        copy = pltpu.make_async_copy(src, dst, sem.at[n_sem])
        n_sem += 1
        copy.start()
        return copy

    piece_cp, w_cp = [], []
    rec_cp = None
    scan_cp = []
    for ri, rnd in enumerate(stage):
        piece_cp += [start(piece_hbm[ri * n_pos + p], piece_buf[ri * n_pos + p]) for p in range(n_pos)]
        w_cp.append(start(w_hbm.at[rnd, 0], w_buf.at[ri]))
        if ri == 0 and has_rec:
            rec_cp = start(rec_hbm, rec_buf)
    if final:
        scan_cp = [start(src, dst) for src, dst in zip(scan_hbm, scan_buf)]

    for ri, rnd in enumerate(stage):
        for p in range(n_pos):
            k = ri * n_pos + p
            piece_cp[k].wait()
            for i in range(local_blocks):
                x = piece_buf[k][:, :, i * side:(i + 1) * side].astype(jnp.float32)
                blocks[p * local_blocks + i] = x.reshape(rows, side).astype(jnp.bfloat16)
        w_cp[ri].wait()
        if ri == 0 and has_rec:
            rec_cp.wait()
        last = ri == n_rounds - 1
        if last and final:
            for copy in scan_cp:
                copy.wait()
            err_buf, surr_buf, lv_buf, la_buf, alpha_buf, rho_buf, beta_buf = scan_buf
        for j in range(local_blocks):
            cols = slice(j * side, (j + 1) * side)
            if ri == 0 and not has_rec:
                acc = jnp.zeros((rows, side), jnp.float32)
            else:
                acc = rec_buf[:, :, cols].reshape(rows, side)
            for k in range(nnz):
                idx = bi_ref[rnd, 0, j, k]
                d = (idx // local_blocks) ^ me
                rel = 0
                for s_, bit in enumerate(reversed(range(bits))):
                    rel = rel | (((d >> bit) & 1) << s_)
                x = blocks[rel * local_blocks + idx % local_blocks]
                acc = acc + jnp.dot(x, w_buf[ri, j, k], preferred_element_type=jnp.float32)
            rec = acc.reshape(steps, batch, side)
            if not last:
                rec_buf[:, :, cols] = rec
                continue
            if not final:
                out_ref[:, :, cols] = rec
                continue
            alpha = alpha_buf[:, cols]
            rho = rho_buf[:, cols]
            beta = beta_buf[:, cols]
            lv_now = lv_buf[:, cols]
            la_now = la_buf[:, cols]
            for t in reversed(range(steps)):
                surr = surr_buf[t, :, cols]
                total = err_buf[t, :, cols] + rec[t] - lv_now + la_now
                cur_ref[t, :, cols] = lv_now.astype(cur_ref.dtype)
                lv_next = alpha * lv_now + surr * total
                la_next = rho * la_now - beta * surr * total
                lv_now, la_now = lv_next, la_next
            lv_out[:, cols] = lv_now
            la_out[:, cols] = la_now


def stage_contrib(block_index, pieces, weights, stage, n_pos, rec, scan_args):
    steps, batch, local = pieces[0].shape
    _, _, local_blocks, nnz, side, _ = weights.shape
    n_rounds = len(stage)
    final = scan_args is not None
    has_rec = rec is not None
    operands = list(pieces) + [weights]
    scratch = [pltpu.VMEM(p.shape, p.dtype) for p in pieces]
    scratch += [
        pltpu.VMEM((n_rounds, local_blocks, nnz, side, side), weights.dtype),
        pltpu.VMEM((n_pos * local_blocks, steps * batch, side), jnp.bfloat16),
    ]
    n_sem = len(pieces) + n_rounds + (1 if has_rec else 0) + (7 if final else 0)
    scratch.append(pltpu.SemaphoreType.DMA((n_sem,)))
    scratch.append(pltpu.VMEM((steps, batch, local), jnp.float32))
    if has_rec:
        operands.append(rec)
    if final:
        err_grad, surrogate, lv_end, la_end, alpha, rho, beta = scan_args
        rows = [a.reshape(1, local) for a in (alpha, rho, beta)]
        extra = [err_grad, surrogate, lv_end, la_end] + rows
        operands += extra
        scratch += [pltpu.VMEM(a.shape, a.dtype) for a in extra]
        out_specs = (VMEM, VMEM, VMEM)
        out_shape = (
            jax.ShapeDtypeStruct((steps, batch, local), jnp.bfloat16),
            jax.ShapeDtypeStruct((batch, local), jnp.float32),
            jax.ShapeDtypeStruct((batch, local), jnp.float32),
        )
    else:
        out_specs = VMEM
        out_shape = jax.ShapeDtypeStruct((steps, batch, local), jnp.float32)
    kernel = functools.partial(
        stage_kernel, n_pieces=len(pieces), stage=tuple(stage), n_pos=n_pos,
        final=final, has_rec=has_rec,
    )
    return pl.pallas_call(
        kernel,
        in_specs=[SMEM] + [ANY] * len(operands),
        out_specs=out_specs,
        scratch_shapes=scratch,
        out_shape=out_shape,
    )(block_index, *operands)


def per_device(
    window, err_grad, surrogate, lv_end, la_end, alpha, rho, beta, weights, block_index, delays
):
    steps = err_grad.shape[0]
    local_neurons = err_grad.shape[2]
    block_side = weights.shape[-1]
    local_blocks = local_neurons // block_side
    rounds = weights.shape[0]
    levels = lax.axis_size("area").bit_length() - 1
    nbits = lax.axis_size("neuron").bit_length() - 1
    n_pos = 1 << nbits
    slices = send_slices(window, delays, rounds, levels, steps)
    stages = [list(range(f, min(f + 2, rounds))) for f in range(0, rounds, 2)]
    arrived = []
    gate = None
    for stage in stages:
        pieces = [slices[rnd] for rnd in stage]
        if gate is not None:
            pieces, _ = lax.optimization_barrier((pieces, gate))
        got = [swap(piece, "area", 1 << (rnd % levels)) for piece, rnd in zip(pieces, stage)]
        arrived += got
        gate = got
    rec = None
    for si, stage in enumerate(stages):
        chunks = []
        for rnd in stage:
            chunks += gather_neuron(arrived[rnd], rec)
        scan_args = None
        if si == len(stages) - 1:
            scan_args = (err_grad, surrogate, lv_end, la_end, alpha, rho, beta)
        rec = stage_contrib(block_index, chunks, weights, stage, n_pos, rec, scan_args)
    return rec


def solution(mesh):
    placed = (
        P(None, "groups", ("area", "neuron")),
        P(None, "groups", ("area", "neuron")),
        P(None, "groups", ("area", "neuron")),
        P("groups", ("area", "neuron")),
        P("groups", ("area", "neuron")),
        P(("area", "neuron")),
        P(("area", "neuron")),
        P(("area", "neuron")),
        P(None, "area", "neuron", None, None, None),
        P(None, "area", "neuron", None),
        P(),
    )
    return jax.shard_map(
        per_device,
        mesh=mesh,
        in_specs=placed,
        out_specs=(
            P(None, "groups", ("area", "neuron")),
            P("groups", ("area", "neuron")),
            P("groups", ("area", "neuron")),
        ),
        check_vma=False,
    )
```

```python
import functools

import jax
import jax.numpy as jnp
from jax import lax
from jax.experimental import pallas as pl
from jax.experimental.pallas import tpu as pltpu
from jax.sharding import PartitionSpec as P

ANY = pl.BlockSpec(memory_space=pl.ANY)
SMEM = pl.BlockSpec(memory_space=pltpu.SMEM)
VMEM = pl.BlockSpec(memory_space=pltpu.VMEM)


def swap(value, axis, mask):
    pairs = [(source, source ^ mask) for source in range(lax.axis_size(axis))]
    return lax.ppermute(value, axis, pairs)


def slice_kernel(delays_ref, window_ref, *outs, levels, steps, n_halves):
    me = lax.axis_index("area")
    width = outs[0].shape[-1]
    for n, out in enumerate(outs):
        rnd, h = divmod(n, n_halves)
        start = delays_ref[rnd, me ^ (1 << (rnd % levels))] - steps
        out[...] = window_ref[pl.ds(start, steps), :, h * width:(h + 1) * width]


def send_slices(window, delays, rounds, levels, steps, n_halves):
    shape = (steps,) + window.shape[1:-1] + (window.shape[-1] // n_halves,)
    kernel = functools.partial(slice_kernel, levels=levels, steps=steps, n_halves=n_halves)
    n_out = rounds * n_halves
    return pl.pallas_call(
        kernel,
        in_specs=[SMEM, VMEM],
        out_specs=[VMEM] * n_out,
        out_shape=[jax.ShapeDtypeStruct(shape, window.dtype)] * n_out,
    )(delays, window)


def gather_neuron(piece, gate=None):
    bits = lax.axis_size("neuron").bit_length() - 1
    held = [piece]
    for bit in reversed(range(bits)):
        if bit == 0 and gate is not None:
            held, _ = lax.optimization_barrier((held, gate))
        held = held + [swap(chunk, "neuron", 1 << bit) for chunk in held]
    return held


def stage_kernel(bi_ref, *refs, n_pieces, stage, n_pos, n_halves, final, has_rec):
    n_rounds = len(stage)
    it = iter(refs)
    piece_hbm = [next(it) for _ in range(n_pieces)]
    w_hbm = next(it)
    rec_hbm = next(it) if has_rec else None
    if final:
        scan_hbm = [next(it) for _ in range(7)]
        cur_ref, lv_out, la_out = next(it), next(it), next(it)
    else:
        out_ref = next(it)
    piece_buf = [next(it) for _ in range(n_pieces)]
    w_buf = next(it)
    blocks = next(it)
    sem = next(it)
    rec_buf = next(it)
    if final:
        scan_buf = [next(it) for _ in range(7)]

    steps, batch, width = piece_hbm[0].shape
    local_blocks, nnz, side = w_buf.shape[1], w_buf.shape[2], w_buf.shape[3]
    rows = steps * batch
    bits = n_pos.bit_length() - 1
    me = lax.axis_index("neuron")
    n_sem = 0

    def start(src, dst):
        nonlocal n_sem
        copy = pltpu.make_async_copy(src, dst, sem.at[n_sem])
        n_sem += 1
        copy.start()
        return copy

    piece_cp, w_cp = [], []
    rec_cp = None
    scan_cp = []
    per_round = n_pos * n_halves
    for ri, rnd in enumerate(stage):
        piece_cp += [start(piece_hbm[ri * per_round + q], piece_buf[ri * per_round + q])
                     for q in range(per_round)]
        w_cp.append(start(w_hbm.at[rnd, 0], w_buf.at[ri]))
        if ri == 0 and has_rec:
            rec_cp = start(rec_hbm, rec_buf)
    if final:
        scan_cp = [start(src, dst) for src, dst in zip(scan_hbm, scan_buf)]

    for ri, rnd in enumerate(stage):
        per_half = local_blocks // n_halves
        for p in range(n_pos):
            for h in range(n_halves):
                k = (ri * n_pos + p) * n_halves + h
                piece_cp[k].wait()
                for i in range(per_half):
                    x = piece_buf[k][:, :, i * side:(i + 1) * side].astype(jnp.float32)
                    x = x.reshape(rows, side).astype(jnp.bfloat16)
                    blocks[p * local_blocks + h * per_half + i] = x
        w_cp[ri].wait()
        if ri == 0 and has_rec:
            rec_cp.wait()
        last = ri == n_rounds - 1
        if last and final:
            for copy in scan_cp:
                copy.wait()
            err_buf, surr_buf, lv_buf, la_buf, alpha_buf, rho_buf, beta_buf = scan_buf
        for j in range(local_blocks):
            cols = slice(j * side, (j + 1) * side)
            if ri == 0 and not has_rec:
                acc = jnp.zeros((rows, side), jnp.float32)
            else:
                acc = rec_buf[:, :, cols].reshape(rows, side)
            for k in range(nnz):
                idx = bi_ref[rnd, 0, j, k]
                d = (idx // local_blocks) ^ me
                rel = 0
                for s_, bit in enumerate(reversed(range(bits))):
                    rel = rel | (((d >> bit) & 1) << s_)
                x = blocks[rel * local_blocks + idx % local_blocks]
                acc = acc + jnp.dot(x, w_buf[ri, j, k], preferred_element_type=jnp.float32)
            rec = acc.reshape(steps, batch, side)
            if not last:
                rec_buf[:, :, cols] = rec
                continue
            if not final:
                out_ref[:, :, cols] = rec
                continue
            alpha = alpha_buf[:, cols]
            rho = rho_buf[:, cols]
            beta = beta_buf[:, cols]
            lv_now = lv_buf[:, cols]
            la_now = la_buf[:, cols]
            for t in reversed(range(steps)):
                surr = surr_buf[t, :, cols]
                total = err_buf[t, :, cols] + rec[t] - lv_now + la_now
                cur_ref[t, :, cols] = lv_now.astype(cur_ref.dtype)
                lv_next = alpha * lv_now + surr * total
                la_next = rho * la_now - beta * surr * total
                lv_now, la_now = lv_next, la_next
            lv_out[:, cols] = lv_now
            la_out[:, cols] = la_now


def stage_contrib(block_index, pieces, weights, stage, n_pos, n_halves, rec, scan_args):
    steps, batch, width = pieces[0].shape
    local = width * n_halves
    _, _, local_blocks, nnz, side, _ = weights.shape
    n_rounds = len(stage)
    final = scan_args is not None
    has_rec = rec is not None
    operands = list(pieces) + [weights]
    scratch = [pltpu.VMEM(p.shape, p.dtype) for p in pieces]
    scratch += [
        pltpu.VMEM((n_rounds, local_blocks, nnz, side, side), weights.dtype),
        pltpu.VMEM((n_pos * local_blocks, steps * batch, side), jnp.bfloat16),
    ]
    n_sem = len(pieces) + n_rounds + (1 if has_rec else 0) + (7 if final else 0)
    scratch.append(pltpu.SemaphoreType.DMA((n_sem,)))
    scratch.append(pltpu.VMEM((steps, batch, local), jnp.float32))
    if has_rec:
        operands.append(rec)
    if final:
        err_grad, surrogate, lv_end, la_end, alpha, rho, beta = scan_args
        rows = [a.reshape(1, local) for a in (alpha, rho, beta)]
        extra = [err_grad, surrogate, lv_end, la_end] + rows
        operands += extra
        scratch += [pltpu.VMEM(a.shape, a.dtype) for a in extra]
        out_specs = (VMEM, VMEM, VMEM)
        out_shape = (
            jax.ShapeDtypeStruct((steps, batch, local), jnp.bfloat16),
            jax.ShapeDtypeStruct((batch, local), jnp.float32),
            jax.ShapeDtypeStruct((batch, local), jnp.float32),
        )
    else:
        out_specs = VMEM
        out_shape = jax.ShapeDtypeStruct((steps, batch, local), jnp.float32)
    kernel = functools.partial(
        stage_kernel, n_pieces=len(pieces), stage=tuple(stage), n_pos=n_pos,
        n_halves=n_halves, final=final, has_rec=has_rec,
    )
    return pl.pallas_call(
        kernel,
        in_specs=[SMEM] + [ANY] * len(operands),
        out_specs=out_specs,
        scratch_shapes=scratch,
        out_shape=out_shape,
    )(block_index, *operands)


def per_device(
    window, err_grad, surrogate, lv_end, la_end, alpha, rho, beta, weights, block_index, delays
):
    steps = err_grad.shape[0]
    local_neurons = err_grad.shape[2]
    block_side = weights.shape[-1]
    local_blocks = local_neurons // block_side
    rounds = weights.shape[0]
    levels = lax.axis_size("area").bit_length() - 1
    nbits = lax.axis_size("neuron").bit_length() - 1
    n_pos = 1 << nbits
    n_halves = 2 if local_blocks % 2 == 0 else 1
    slices = send_slices(window, delays, rounds, levels, steps, n_halves)
    stages = [list(range(f, min(f + 2, rounds))) for f in range(0, rounds, 2)]
    arrived = {}
    gate = None
    for stage in stages:
        for h in range(n_halves):
            pieces = [slices[rnd * n_halves + h] for rnd in stage]
            if gate is not None:
                pieces, _ = lax.optimization_barrier((pieces, gate))
            got = [swap(piece, "area", 1 << (rnd % levels)) for piece, rnd in zip(pieces, stage)]
            for rnd, g in zip(stage, got):
                arrived[(rnd, h)] = g
            gate = got
    rec = None
    for si, stage in enumerate(stages):
        chunks = []
        for rnd in stage:
            halves = [gather_neuron(arrived[(rnd, h)], rec) for h in range(n_halves)]
            chunks += [halves[h][p] for p in range(n_pos) for h in range(n_halves)]
        scan_args = None
        if si == len(stages) - 1:
            scan_args = (err_grad, surrogate, lv_end, la_end, alpha, rho, beta)
        rec = stage_contrib(block_index, chunks, weights, stage, n_pos, n_halves, rec, scan_args)
    return rec


def solution(mesh):
    placed = (
        P(None, "groups", ("area", "neuron")),
        P(None, "groups", ("area", "neuron")),
        P(None, "groups", ("area", "neuron")),
        P("groups", ("area", "neuron")),
        P("groups", ("area", "neuron")),
        P(("area", "neuron")),
        P(("area", "neuron")),
        P(("area", "neuron")),
        P(None, "area", "neuron", None, None, None),
        P(None, "area", "neuron", None),
        P(),
    )
    return jax.shard_map(
        per_device,
        mesh=mesh,
        in_specs=placed,
        out_specs=(
            P(None, "groups", ("area", "neuron")),
            P("groups", ("area", "neuron")),
            P("groups", ("area", "neuron")),
        ),
        check_vma=False,
    )
```

```python
import functools

import jax
import jax.numpy as jnp
from jax import lax
from jax.experimental import pallas as pl
from jax.experimental.pallas import tpu as pltpu
from jax.sharding import PartitionSpec as P

ANY = pl.BlockSpec(memory_space=pl.ANY)
SMEM = pl.BlockSpec(memory_space=pltpu.SMEM)
VMEM = pl.BlockSpec(memory_space=pltpu.VMEM)


def swap(value, axis, mask):
    pairs = [(source, source ^ mask) for source in range(lax.axis_size(axis))]
    return lax.ppermute(value, axis, pairs)


def slice_kernel(delays_ref, window_ref, *outs, levels, steps):
    me = lax.axis_index("area")
    rows, width = outs[0].shape
    side = 128 if width % 128 == 0 else width
    for rnd, out in enumerate(outs):
        start = delays_ref[rnd, me ^ (1 << (rnd % levels))] - steps
        for c in range(0, width, side):
            x = window_ref[pl.ds(start, steps), :, c:c + side].astype(jnp.float32)
            out[:, c:c + side] = x.reshape(rows, side).astype(out.dtype)


def send_slices(window, delays, rounds, levels, steps):
    shape = (steps * window.shape[1], window.shape[2])
    kernel = functools.partial(slice_kernel, levels=levels, steps=steps)
    return pl.pallas_call(
        kernel,
        in_specs=[SMEM, VMEM],
        out_specs=[VMEM] * rounds,
        out_shape=[jax.ShapeDtypeStruct(shape, window.dtype)] * rounds,
    )(delays, window)


def gather_neuron(piece, gate=None):
    bits = lax.axis_size("neuron").bit_length() - 1
    held = [piece]
    for bit in reversed(range(bits)):
        if bit == 0 and gate is not None:
            held, _ = lax.optimization_barrier((held, gate))
        held = held + [swap(chunk, "neuron", 1 << bit) for chunk in held]
    return held


def stage_kernel(bi_ref, *refs, n_pieces, stage, n_pos, final, has_rec):
    n_rounds = len(stage)
    it = iter(refs)
    piece_hbm = [next(it) for _ in range(n_pieces)]
    w_hbm = next(it)
    rec_hbm = next(it) if has_rec else None
    if final:
        scan_hbm = [next(it) for _ in range(7)]
        cur_ref, lv_out, la_out = next(it), next(it), next(it)
    else:
        out_ref = next(it)
    piece_buf = next(it)
    w_buf = next(it)
    sem = next(it)
    rec_buf = next(it)
    if final:
        scan_buf = [next(it) for _ in range(7)]

    steps, batch = rec_buf.shape[0], rec_buf.shape[1]
    local_blocks, nnz, side = w_buf.shape[1], w_buf.shape[2], w_buf.shape[3]
    rows = steps * batch
    bits = n_pos.bit_length() - 1
    me = lax.axis_index("neuron")
    n_sem = 0

    def start(src, dst):
        nonlocal n_sem
        copy = pltpu.make_async_copy(src, dst, sem.at[n_sem])
        n_sem += 1
        copy.start()
        return copy

    piece_cp, w_cp = [], []
    rec_cp = None
    scan_cp = []
    for ri, rnd in enumerate(stage):
        piece_cp += [start(piece_hbm[ri * n_pos + p], piece_buf.at[ri * n_pos + p]) for p in range(n_pos)]
        w_cp.append(start(w_hbm.at[rnd, 0], w_buf.at[ri]))
        if ri == 0 and has_rec:
            rec_cp = start(rec_hbm, rec_buf)
    if final:
        scan_cp = [start(src, dst) for src, dst in zip(scan_hbm, scan_buf)]

    for ri, rnd in enumerate(stage):
        for p in range(n_pos):
            piece_cp[ri * n_pos + p].wait()
        w_cp[ri].wait()
        if ri == 0 and has_rec:
            rec_cp.wait()
        last = ri == n_rounds - 1
        if last and final:
            for copy in scan_cp:
                copy.wait()
            err_buf, surr_buf, lv_buf, la_buf, alpha_buf, rho_buf, beta_buf = scan_buf
        for j in range(local_blocks):
            cols = slice(j * side, (j + 1) * side)
            if ri == 0 and not has_rec:
                acc = jnp.zeros((rows, side), jnp.float32)
            else:
                acc = rec_buf[:, :, cols].reshape(rows, side)
            for k in range(nnz):
                idx = bi_ref[rnd, 0, j, k]
                d = (idx // local_blocks) ^ me
                rel = 0
                for s_, bit in enumerate(reversed(range(bits))):
                    rel = rel | (((d >> bit) & 1) << s_)
                off = pl.multiple_of((idx % local_blocks) * side, side)
                x = piece_buf[ri * n_pos + rel, :, pl.ds(off, side)]
                acc = acc + jnp.dot(x, w_buf[ri, j, k], preferred_element_type=jnp.float32)
            rec = acc.reshape(steps, batch, side)
            if not last:
                rec_buf[:, :, cols] = rec
                continue
            if not final:
                out_ref[:, :, cols] = rec
                continue
            alpha = alpha_buf[:, cols]
            rho = rho_buf[:, cols]
            beta = beta_buf[:, cols]
            lv_now = lv_buf[:, cols]
            la_now = la_buf[:, cols]
            for t in reversed(range(steps)):
                surr = surr_buf[t, :, cols]
                total = err_buf[t, :, cols] + rec[t] - lv_now + la_now
                cur_ref[t, :, cols] = lv_now.astype(cur_ref.dtype)
                lv_next = alpha * lv_now + surr * total
                la_next = rho * la_now - beta * surr * total
                lv_now, la_now = lv_next, la_next
            lv_out[:, cols] = lv_now
            la_out[:, cols] = la_now


def stage_contrib(block_index, pieces, weights, stage, n_pos, rec, scan_args, steps):
    rows, local = pieces[0].shape
    _, _, local_blocks, nnz, side, _ = weights.shape
    batch = rows // steps
    n_rounds = len(stage)
    final = scan_args is not None
    has_rec = rec is not None
    operands = list(pieces) + [weights]
    scratch = [
        pltpu.VMEM((len(pieces), rows, local), pieces[0].dtype),
        pltpu.VMEM((n_rounds, local_blocks, nnz, side, side), weights.dtype),
    ]
    n_sem = len(pieces) + n_rounds + (1 if has_rec else 0) + (7 if final else 0)
    scratch.append(pltpu.SemaphoreType.DMA((n_sem,)))
    scratch.append(pltpu.VMEM((steps, batch, local), jnp.float32))
    if has_rec:
        operands.append(rec)
    if final:
        err_grad, surrogate, lv_end, la_end, alpha, rho, beta = scan_args
        rows = [a.reshape(1, local) for a in (alpha, rho, beta)]
        extra = [err_grad, surrogate, lv_end, la_end] + rows
        operands += extra
        scratch += [pltpu.VMEM(a.shape, a.dtype) for a in extra]
        out_specs = (VMEM, VMEM, VMEM)
        out_shape = (
            jax.ShapeDtypeStruct((steps, batch, local), jnp.bfloat16),
            jax.ShapeDtypeStruct((batch, local), jnp.float32),
            jax.ShapeDtypeStruct((batch, local), jnp.float32),
        )
    else:
        out_specs = VMEM
        out_shape = jax.ShapeDtypeStruct((steps, batch, local), jnp.float32)
    kernel = functools.partial(
        stage_kernel, n_pieces=len(pieces), stage=tuple(stage), n_pos=n_pos,
        final=final, has_rec=has_rec,
    )
    return pl.pallas_call(
        kernel,
        in_specs=[SMEM] + [ANY] * len(operands),
        out_specs=out_specs,
        scratch_shapes=scratch,
        out_shape=out_shape,
    )(block_index, *operands)


def per_device(
    window, err_grad, surrogate, lv_end, la_end, alpha, rho, beta, weights, block_index, delays
):
    steps = err_grad.shape[0]
    local_neurons = err_grad.shape[2]
    block_side = weights.shape[-1]
    local_blocks = local_neurons // block_side
    rounds = weights.shape[0]
    levels = lax.axis_size("area").bit_length() - 1
    nbits = lax.axis_size("neuron").bit_length() - 1
    n_pos = 1 << nbits
    slices = send_slices(window, delays, rounds, levels, steps)
    stages = [list(range(f, min(f + 2, rounds))) for f in range(0, rounds, 2)]
    arrived = []
    gate = None
    for stage in stages:
        pieces = [slices[rnd] for rnd in stage]
        if gate is not None:
            pieces, _ = lax.optimization_barrier((pieces, gate))
        got = [swap(piece, "area", 1 << (rnd % levels)) for piece, rnd in zip(pieces, stage)]
        arrived += got
        gate = got
    rec = None
    for si, stage in enumerate(stages):
        chunks = []
        for rnd in stage:
            chunks += gather_neuron(arrived[rnd], rec)
        scan_args = None
        if si == len(stages) - 1:
            scan_args = (err_grad, surrogate, lv_end, la_end, alpha, rho, beta)
        rec = stage_contrib(block_index, chunks, weights, stage, n_pos, rec, scan_args, steps)
    return rec


def solution(mesh):
    placed = (
        P(None, "groups", ("area", "neuron")),
        P(None, "groups", ("area", "neuron")),
        P(None, "groups", ("area", "neuron")),
        P("groups", ("area", "neuron")),
        P("groups", ("area", "neuron")),
        P(("area", "neuron")),
        P(("area", "neuron")),
        P(("area", "neuron")),
        P(None, "area", "neuron", None, None, None),
        P(None, "area", "neuron", None),
        P(),
    )
    return jax.shard_map(
        per_device,
        mesh=mesh,
        in_specs=placed,
        out_specs=(
            P(None, "groups", ("area", "neuron")),
            P("groups", ("area", "neuron")),
            P("groups", ("area", "neuron")),
        ),
        check_vma=False,
    )
```

```python
import functools

import jax
import jax.numpy as jnp
from jax import lax
from jax.experimental import pallas as pl
from jax.experimental.pallas import tpu as pltpu
from jax.sharding import PartitionSpec as P

ANY = pl.BlockSpec(memory_space=pl.ANY)
SMEM = pl.BlockSpec(memory_space=pltpu.SMEM)
VMEM = pl.BlockSpec(memory_space=pltpu.VMEM)


def swap(value, axis, mask):
    pairs = [(source, source ^ mask) for source in range(lax.axis_size(axis))]
    return lax.ppermute(value, axis, pairs)


def slice_kernel(delays_ref, window_ref, *outs, levels, steps):
    me = lax.axis_index("area")
    rows, width = outs[0].shape
    side = 128 if width % 128 == 0 else width
    for rnd, out in enumerate(outs):
        start = delays_ref[rnd, me ^ (1 << (rnd % levels))] - steps
        for c in range(0, width, side):
            x = window_ref[pl.ds(start, steps), :, c:c + side].astype(jnp.float32)
            out[:, c:c + side] = x.reshape(rows, side).astype(out.dtype)


def send_slices(window, delays, rounds, levels, steps):
    shape = (steps * window.shape[1], window.shape[2])
    kernel = functools.partial(slice_kernel, levels=levels, steps=steps)
    return pl.pallas_call(
        kernel,
        in_specs=[SMEM, VMEM],
        out_specs=[VMEM] * rounds,
        out_shape=[jax.ShapeDtypeStruct(shape, window.dtype)] * rounds,
    )(delays, window)


def gather_neuron(piece, gate=None):
    bits = lax.axis_size("neuron").bit_length() - 1
    held = [piece]
    for bit in reversed(range(bits)):
        if bit == 0 and gate is not None:
            held, _ = lax.optimization_barrier((held, gate))
        held = held + [swap(chunk, "neuron", 1 << bit) for chunk in held]
    return held


def stage_kernel(bi_ref, *refs, n_pieces, stage, n_pos, final, has_rec):
    n_rounds = len(stage)
    it = iter(refs)
    piece_hbm = [next(it) for _ in range(n_pieces)]
    w_hbm = next(it)
    rec_hbm = next(it) if has_rec else None
    if final:
        scan_hbm = [next(it) for _ in range(7)]
        cur_ref, lv_out, la_out = next(it), next(it), next(it)
    else:
        out_ref = next(it)
    piece_buf = next(it)
    w_buf = next(it)
    sem = next(it)
    rec_buf = next(it)
    if final:
        scan_buf = [next(it) for _ in range(7)]

    steps, batch = rec_buf.shape[0], rec_buf.shape[1]
    local_blocks, nnz, side = w_buf.shape[1], w_buf.shape[2], w_buf.shape[3]
    rows = steps * batch
    bits = n_pos.bit_length() - 1
    me = lax.axis_index("neuron")
    n_sem = 0

    def start(src, dst):
        nonlocal n_sem
        copy = pltpu.make_async_copy(src, dst, sem.at[n_sem])
        n_sem += 1
        copy.start()
        return copy

    piece_cp, w_cp = [], []
    rec_cp = None
    scan_cp = []
    for ri, rnd in enumerate(stage):
        piece_cp += [start(piece_hbm[ri * n_pos + p], piece_buf.at[ri * n_pos + p]) for p in range(n_pos)]
        w_cp.append(start(w_hbm.at[rnd, 0], w_buf.at[ri]))
        if ri == 0 and has_rec:
            rec_cp = start(rec_hbm, rec_buf)
    if final:
        scan_cp = [start(src, dst) for src, dst in zip(scan_hbm, scan_buf)]

    for ri, rnd in enumerate(stage):
        for p in range(n_pos):
            piece_cp[ri * n_pos + p].wait()
        w_cp[ri].wait()
        if ri == 0 and has_rec:
            rec_cp.wait()
        last = ri == n_rounds - 1
        if last and final:
            for copy in scan_cp:
                copy.wait()
            err_buf, surr_buf, lv_buf, la_buf, alpha_buf, rho_buf, beta_buf = scan_buf
        for j in range(local_blocks):
            cols = slice(j * side, (j + 1) * side)
            if ri == 0 and not has_rec:
                acc = jnp.zeros((rows, side), jnp.float32)
            else:
                acc = rec_buf[:, :, cols].reshape(rows, side)
            for k in range(nnz):
                idx = bi_ref[rnd, 0, j, k]
                d = (idx // local_blocks) ^ me
                rel = 0
                for s_, bit in enumerate(reversed(range(bits))):
                    rel = rel | (((d >> bit) & 1) << s_)
                off = pl.multiple_of((idx % local_blocks) * side, side)
                x = piece_buf[ri * n_pos + rel, :, pl.ds(off, side)]
                acc = acc + jnp.dot(x, w_buf[ri, j, k], preferred_element_type=jnp.float32)
            rec = acc.reshape(steps, batch, side)
            if not last:
                rec_buf[:, :, cols] = rec
                continue
            if not final:
                out_ref[:, :, cols] = rec
                continue
            alpha = alpha_buf[:, cols]
            rho = rho_buf[:, cols]
            beta = beta_buf[:, cols]
            lv_now = lv_buf[:, cols]
            la_now = la_buf[:, cols]
            for t in reversed(range(steps)):
                surr = surr_buf[t, :, cols]
                total = err_buf[t, :, cols] + rec[t] - lv_now + la_now
                cur_ref[t, :, cols] = lv_now.astype(cur_ref.dtype)
                lv_next = alpha * lv_now + surr * total
                la_next = rho * la_now - beta * surr * total
                lv_now, la_now = lv_next, la_next
            lv_out[:, cols] = lv_now
            la_out[:, cols] = la_now


def stage_contrib(block_index, pieces, weights, stage, n_pos, rec, scan_args, steps):
    rows, local = pieces[0].shape
    _, _, local_blocks, nnz, side, _ = weights.shape
    batch = rows // steps
    n_rounds = len(stage)
    final = scan_args is not None
    has_rec = rec is not None
    operands = list(pieces) + [weights]
    scratch = [
        pltpu.VMEM((len(pieces), rows, local), pieces[0].dtype),
        pltpu.VMEM((n_rounds, local_blocks, nnz, side, side), weights.dtype),
    ]
    n_sem = len(pieces) + n_rounds + (1 if has_rec else 0) + (7 if final else 0)
    scratch.append(pltpu.SemaphoreType.DMA((n_sem,)))
    scratch.append(pltpu.VMEM((steps, batch, local), jnp.float32))
    if has_rec:
        operands.append(rec)
    if final:
        err_grad, surrogate, lv_end, la_end, alpha, rho, beta = scan_args
        rows = [a.reshape(1, local) for a in (alpha, rho, beta)]
        extra = [err_grad, surrogate, lv_end, la_end] + rows
        operands += extra
        scratch += [pltpu.VMEM(a.shape, a.dtype) for a in extra]
        out_specs = (VMEM, VMEM, VMEM)
        out_shape = (
            jax.ShapeDtypeStruct((steps, batch, local), jnp.bfloat16),
            jax.ShapeDtypeStruct((batch, local), jnp.float32),
            jax.ShapeDtypeStruct((batch, local), jnp.float32),
        )
    else:
        out_specs = VMEM
        out_shape = jax.ShapeDtypeStruct((steps, batch, local), jnp.float32)
    kernel = functools.partial(
        stage_kernel, n_pieces=len(pieces), stage=tuple(stage), n_pos=n_pos,
        final=final, has_rec=has_rec,
    )
    pinned = [final and i > len(pieces) + has_rec for i in range(len(operands))]
    specs = [VMEM if p else ANY for p in pinned]
    operands = [pltpu.with_memory_space_constraint(x, pltpu.VMEM) if p else x
                for x, p in zip(operands, pinned)]
    return pl.pallas_call(
        kernel,
        in_specs=[SMEM] + specs,
        out_specs=out_specs,
        scratch_shapes=scratch,
        out_shape=out_shape,
    )(block_index, *operands)


def per_device(
    window, err_grad, surrogate, lv_end, la_end, alpha, rho, beta, weights, block_index, delays
):
    steps = err_grad.shape[0]
    local_neurons = err_grad.shape[2]
    block_side = weights.shape[-1]
    local_blocks = local_neurons // block_side
    rounds = weights.shape[0]
    levels = lax.axis_size("area").bit_length() - 1
    nbits = lax.axis_size("neuron").bit_length() - 1
    n_pos = 1 << nbits
    slices = send_slices(window, delays, rounds, levels, steps)
    stages = [list(range(f, min(f + 2, rounds))) for f in range(0, rounds, 2)]
    arrived = []
    gate = None
    for stage in stages:
        pieces = [slices[rnd] for rnd in stage]
        if gate is not None:
            pieces, _ = lax.optimization_barrier((pieces, gate))
        got = [swap(piece, "area", 1 << (rnd % levels)) for piece, rnd in zip(pieces, stage)]
        arrived += got
        gate = got
    rec = None
    for si, stage in enumerate(stages):
        chunks = []
        for rnd in stage:
            chunks += gather_neuron(arrived[rnd], rec)
        scan_args = None
        if si == len(stages) - 1:
            scan_args = (err_grad, surrogate, lv_end, la_end, alpha, rho, beta)
        rec = stage_contrib(block_index, chunks, weights, stage, n_pos, rec, scan_args, steps)
    return rec


def solution(mesh):
    placed = (
        P(None, "groups", ("area", "neuron")),
        P(None, "groups", ("area", "neuron")),
        P(None, "groups", ("area", "neuron")),
        P("groups", ("area", "neuron")),
        P("groups", ("area", "neuron")),
        P(("area", "neuron")),
        P(("area", "neuron")),
        P(("area", "neuron")),
        P(None, "area", "neuron", None, None, None),
        P(None, "area", "neuron", None),
        P(),
    )
    return jax.shard_map(
        per_device,
        mesh=mesh,
        in_specs=placed,
        out_specs=(
            P(None, "groups", ("area", "neuron")),
            P("groups", ("area", "neuron")),
            P("groups", ("area", "neuron")),
        ),
        check_vma=False,
    )
```

```python
import functools

import jax
import jax.numpy as jnp
from jax import lax
from jax.experimental import pallas as pl
from jax.experimental.pallas import tpu as pltpu
from jax.sharding import PartitionSpec as P

ANY = pl.BlockSpec(memory_space=pl.ANY)
SMEM = pl.BlockSpec(memory_space=pltpu.SMEM)
VMEM = pl.BlockSpec(memory_space=pltpu.VMEM)


def swap(value, axis, mask):
    pairs = [(source, source ^ mask) for source in range(lax.axis_size(axis))]
    return lax.ppermute(value, axis, pairs)


def slice_kernel(delays_ref, window_ref, *outs, rounds, levels, steps):
    me = lax.axis_index("area")
    rows, width = outs[0].shape
    side = 128 if width % 128 == 0 else width
    for rnd, out in zip(rounds, outs):
        start = delays_ref[rnd, me ^ (1 << (rnd % levels))] - steps
        for c in range(0, width, side):
            x = window_ref[pl.ds(start, steps), :, c:c + side].astype(jnp.float32)
            out[:, c:c + side] = x.reshape(rows, side).astype(out.dtype)


def send_slices(window, delays, rounds, levels, steps):
    shape = (steps * window.shape[1], window.shape[2])
    kernel = functools.partial(slice_kernel, rounds=tuple(rounds), levels=levels, steps=steps)
    return pl.pallas_call(
        kernel,
        in_specs=[SMEM, VMEM],
        out_specs=[VMEM] * len(rounds),
        out_shape=[jax.ShapeDtypeStruct(shape, window.dtype)] * len(rounds),
    )(delays, window)


def gather_neuron(piece, gate=None):
    bits = lax.axis_size("neuron").bit_length() - 1
    held = [piece]
    for bit in reversed(range(bits)):
        if bit == 0 and gate is not None:
            held, _ = lax.optimization_barrier((held, gate))
        held = held + [swap(chunk, "neuron", 1 << bit) for chunk in held]
    return held


def stage_kernel(bi_ref, *refs, n_pieces, stage, n_pos, final, has_rec):
    n_rounds = len(stage)
    it = iter(refs)
    piece_hbm = [next(it) for _ in range(n_pieces)]
    w_hbm = next(it)
    rec_hbm = next(it) if has_rec else None
    if final:
        scan_hbm = [next(it) for _ in range(7)]
        cur_ref, lv_out, la_out = next(it), next(it), next(it)
    else:
        out_ref = next(it)
    piece_buf = next(it)
    w_buf = next(it)
    sem = next(it)
    rec_buf = next(it)
    if final:
        scan_buf = [next(it) for _ in range(7)]

    steps, batch = rec_buf.shape[0], rec_buf.shape[1]
    local_blocks, nnz, side = w_buf.shape[1], w_buf.shape[2], w_buf.shape[3]
    rows = steps * batch
    bits = n_pos.bit_length() - 1
    me = lax.axis_index("neuron")
    n_sem = 0

    def start(src, dst):
        nonlocal n_sem
        copy = pltpu.make_async_copy(src, dst, sem.at[n_sem])
        n_sem += 1
        copy.start()
        return copy

    piece_cp, w_cp = [], []
    rec_cp = None
    scan_cp = []
    for ri, rnd in enumerate(stage):
        piece_cp += [start(piece_hbm[ri * n_pos + p], piece_buf.at[ri * n_pos + p]) for p in range(n_pos)]
        w_cp.append(start(w_hbm.at[rnd, 0], w_buf.at[ri]))
        if ri == 0 and has_rec:
            rec_cp = start(rec_hbm, rec_buf)
    if final:
        scan_cp = [start(src, dst) for src, dst in zip(scan_hbm, scan_buf)]

    for ri, rnd in enumerate(stage):
        for p in range(n_pos):
            piece_cp[ri * n_pos + p].wait()
        w_cp[ri].wait()
        if ri == 0 and has_rec:
            rec_cp.wait()
        last = ri == n_rounds - 1
        if last and final:
            for copy in scan_cp:
                copy.wait()
            err_buf, surr_buf, lv_buf, la_buf, alpha_buf, rho_buf, beta_buf = scan_buf
        for j in range(local_blocks):
            cols = slice(j * side, (j + 1) * side)
            if ri == 0 and not has_rec:
                acc = jnp.zeros((rows, side), jnp.float32)
            else:
                acc = rec_buf[:, :, cols].reshape(rows, side)
            for k in range(nnz):
                idx = bi_ref[rnd, 0, j, k]
                d = (idx // local_blocks) ^ me
                rel = 0
                for s_, bit in enumerate(reversed(range(bits))):
                    rel = rel | (((d >> bit) & 1) << s_)
                off = pl.multiple_of((idx % local_blocks) * side, side)
                x = piece_buf[ri * n_pos + rel, :, pl.ds(off, side)]
                acc = acc + jnp.dot(x, w_buf[ri, j, k], preferred_element_type=jnp.float32)
            rec = acc.reshape(steps, batch, side)
            if not last:
                rec_buf[:, :, cols] = rec
                continue
            if not final:
                out_ref[:, :, cols] = rec
                continue
            alpha = alpha_buf[:, cols]
            rho = rho_buf[:, cols]
            beta = beta_buf[:, cols]
            lv_now = lv_buf[:, cols]
            la_now = la_buf[:, cols]
            for t in reversed(range(steps)):
                surr = surr_buf[t, :, cols]
                total = err_buf[t, :, cols] + rec[t] - lv_now + la_now
                cur_ref[t, :, cols] = lv_now.astype(cur_ref.dtype)
                lv_next = alpha * lv_now + surr * total
                la_next = rho * la_now - beta * surr * total
                lv_now, la_now = lv_next, la_next
            lv_out[:, cols] = lv_now
            la_out[:, cols] = la_now


def stage_contrib(block_index, pieces, weights, stage, n_pos, rec, scan_args, steps):
    rows, local = pieces[0].shape
    _, _, local_blocks, nnz, side, _ = weights.shape
    batch = rows // steps
    n_rounds = len(stage)
    final = scan_args is not None
    has_rec = rec is not None
    operands = list(pieces) + [weights]
    scratch = [
        pltpu.VMEM((len(pieces), rows, local), pieces[0].dtype),
        pltpu.VMEM((n_rounds, local_blocks, nnz, side, side), weights.dtype),
    ]
    n_sem = len(pieces) + n_rounds + (1 if has_rec else 0) + (7 if final else 0)
    scratch.append(pltpu.SemaphoreType.DMA((n_sem,)))
    scratch.append(pltpu.VMEM((steps, batch, local), jnp.float32))
    if has_rec:
        operands.append(rec)
    if final:
        err_grad, surrogate, lv_end, la_end, alpha, rho, beta = scan_args
        rows = [a.reshape(1, local) for a in (alpha, rho, beta)]
        extra = [err_grad, surrogate, lv_end, la_end] + rows
        operands += extra
        scratch += [pltpu.VMEM(a.shape, a.dtype) for a in extra]
        out_specs = (VMEM, VMEM, VMEM)
        out_shape = (
            jax.ShapeDtypeStruct((steps, batch, local), jnp.bfloat16),
            jax.ShapeDtypeStruct((batch, local), jnp.float32),
            jax.ShapeDtypeStruct((batch, local), jnp.float32),
        )
    else:
        out_specs = VMEM
        out_shape = jax.ShapeDtypeStruct((steps, batch, local), jnp.float32)
    kernel = functools.partial(
        stage_kernel, n_pieces=len(pieces), stage=tuple(stage), n_pos=n_pos,
        final=final, has_rec=has_rec,
    )
    pinned = [final and i > len(pieces) + has_rec for i in range(len(operands))]
    specs = [VMEM if p else ANY for p in pinned]
    operands = [pltpu.with_memory_space_constraint(x, pltpu.VMEM) if p else x
                for x, p in zip(operands, pinned)]
    return pl.pallas_call(
        kernel,
        in_specs=[SMEM] + specs,
        out_specs=out_specs,
        scratch_shapes=scratch,
        out_shape=out_shape,
    )(block_index, *operands)


def per_device(
    window, err_grad, surrogate, lv_end, la_end, alpha, rho, beta, weights, block_index, delays
):
    steps = err_grad.shape[0]
    local_neurons = err_grad.shape[2]
    block_side = weights.shape[-1]
    local_blocks = local_neurons // block_side
    rounds = weights.shape[0]
    levels = lax.axis_size("area").bit_length() - 1
    nbits = lax.axis_size("neuron").bit_length() - 1
    n_pos = 1 << nbits
    stages = [list(range(f, min(f + 2, rounds))) for f in range(0, rounds, 2)]
    arrived = []
    gate = None
    for stage in stages:
        pieces = send_slices(window, delays, stage, levels, steps)
        if gate is not None:
            pieces, _ = lax.optimization_barrier((pieces, gate))
        got = [swap(piece, "area", 1 << (rnd % levels)) for piece, rnd in zip(pieces, stage)]
        arrived += got
        gate = got
    rec = None
    for si, stage in enumerate(stages):
        chunks = []
        for rnd in stage:
            chunks += gather_neuron(arrived[rnd], rec)
        scan_args = None
        if si == len(stages) - 1:
            scan_args = (err_grad, surrogate, lv_end, la_end, alpha, rho, beta)
        rec = stage_contrib(block_index, chunks, weights, stage, n_pos, rec, scan_args, steps)
    return rec


def solution(mesh):
    placed = (
        P(None, "groups", ("area", "neuron")),
        P(None, "groups", ("area", "neuron")),
        P(None, "groups", ("area", "neuron")),
        P("groups", ("area", "neuron")),
        P("groups", ("area", "neuron")),
        P(("area", "neuron")),
        P(("area", "neuron")),
        P(("area", "neuron")),
        P(None, "area", "neuron", None, None, None),
        P(None, "area", "neuron", None),
        P(),
    )
    return jax.shard_map(
        per_device,
        mesh=mesh,
        in_specs=placed,
        out_specs=(
            P(None, "groups", ("area", "neuron")),
            P("groups", ("area", "neuron")),
            P("groups", ("area", "neuron")),
        ),
        check_vma=False,
    )
```

```python
import functools

import jax
import jax.numpy as jnp
from jax import lax
from jax.experimental import pallas as pl
from jax.experimental.pallas import tpu as pltpu
from jax.sharding import PartitionSpec as P

ANY = pl.BlockSpec(memory_space=pl.ANY)
SMEM = pl.BlockSpec(memory_space=pltpu.SMEM)
VMEM = pl.BlockSpec(memory_space=pltpu.VMEM)


def swap(value, axis, mask):
    pairs = [(source, source ^ mask) for source in range(lax.axis_size(axis))]
    return lax.ppermute(value, axis, pairs)


def slice_kernel(delays_ref, window_ref, *outs, rounds, levels, steps):
    me = lax.axis_index("area")
    rows, width = outs[0].shape
    side = 128 if width % 128 == 0 else width
    for rnd, out in zip(rounds, outs):
        start = delays_ref[rnd, me ^ (1 << (rnd % levels))] - steps
        for c in range(0, width, side):
            x = window_ref[pl.ds(start, steps), :, c:c + side].astype(jnp.float32)
            out[:, c:c + side] = x.reshape(rows, side).astype(out.dtype)


def send_slices(window, delays, rounds, levels, steps):
    shape = (steps * window.shape[1], window.shape[2])
    kernel = functools.partial(slice_kernel, rounds=tuple(rounds), levels=levels, steps=steps)
    return pl.pallas_call(
        kernel,
        in_specs=[SMEM, VMEM],
        out_specs=[VMEM] * len(rounds),
        out_shape=[jax.ShapeDtypeStruct(shape, window.dtype)] * len(rounds),
    )(delays, window)


def gather_neuron(piece, gate=None):
    bits = lax.axis_size("neuron").bit_length() - 1
    held = [piece]
    for bit in reversed(range(bits)):
        if bit == 0 and gate is not None:
            held, _ = lax.optimization_barrier((held, gate))
        held = held + [swap(chunk, "neuron", 1 << bit) for chunk in held]
    return held


def stage_kernel(bi_ref, *refs, n_pieces, stage, n_pos, final, has_rec):
    n_rounds = len(stage)
    it = iter(refs)
    piece_hbm = [next(it) for _ in range(n_pieces)]
    w_hbm = next(it)
    rec_hbm = next(it) if has_rec else None
    if final:
        scan_hbm = [next(it) for _ in range(7)]
        cur_ref, lv_out, la_out = next(it), next(it), next(it)
    else:
        out_ref = next(it)
    piece_buf = next(it)
    w_buf = next(it)
    sem = next(it)
    rec_buf = next(it)
    if final:
        scan_buf = [next(it) for _ in range(7)]

    steps, batch = rec_buf.shape[0], rec_buf.shape[1]
    local_blocks, nnz, side = w_buf.shape[1], w_buf.shape[2], w_buf.shape[3]
    rows = steps * batch
    bits = n_pos.bit_length() - 1
    me = lax.axis_index("neuron")
    n_sem = 0

    def start(src, dst):
        nonlocal n_sem
        copy = pltpu.make_async_copy(src, dst, sem.at[n_sem])
        n_sem += 1
        copy.start()
        return copy

    piece_cp, w_cp = [], []
    rec_cp = None
    scan_cp = []
    for ri, rnd in enumerate(stage):
        piece_cp += [start(piece_hbm[ri * n_pos + p], piece_buf.at[ri * n_pos + p]) for p in range(n_pos)]
        w_cp.append(start(w_hbm.at[rnd, 0], w_buf.at[ri]))
        if ri == 0 and has_rec:
            rec_cp = start(rec_hbm, rec_buf)
    if final:
        scan_cp = [start(src, dst) for src, dst in zip(scan_hbm, scan_buf)]

    for ri, rnd in enumerate(stage):
        for p in range(n_pos):
            piece_cp[ri * n_pos + p].wait()
        w_cp[ri].wait()
        if ri == 0 and has_rec:
            rec_cp.wait()
        last = ri == n_rounds - 1
        if last and final:
            for copy in scan_cp:
                copy.wait()
            err_buf, surr_buf, lv_buf, la_buf, alpha_buf, rho_buf, beta_buf = scan_buf
        for j in range(local_blocks):
            cols = slice(j * side, (j + 1) * side)
            if ri == 0 and not has_rec:
                acc = jnp.zeros((rows, side), jnp.float32)
            else:
                acc = rec_buf[:, :, cols].reshape(rows, side)
            for k in range(nnz):
                idx = bi_ref[rnd, 0, j, k]
                d = (idx // local_blocks) ^ me
                rel = 0
                for s_, bit in enumerate(reversed(range(bits))):
                    rel = rel | (((d >> bit) & 1) << s_)
                off = pl.multiple_of((idx % local_blocks) * side, side)
                x = piece_buf[ri * n_pos + rel, :, pl.ds(off, side)]
                acc = acc + jnp.dot(x, w_buf[ri, j, k], preferred_element_type=jnp.float32)
            rec = acc.reshape(steps, batch, side)
            if not last:
                rec_buf[:, :, cols] = rec
                continue
            if not final:
                out_ref[:, :, cols] = rec
                continue
            alpha = alpha_buf[:, cols]
            rho = rho_buf[:, cols]
            beta = beta_buf[:, cols]
            lv_now = lv_buf[:, cols]
            la_now = la_buf[:, cols]
            for t in reversed(range(steps)):
                surr = surr_buf[t, :, cols]
                total = err_buf[t, :, cols] + rec[t] - lv_now + la_now
                cur_ref[t, :, cols] = lv_now.astype(cur_ref.dtype)
                lv_next = alpha * lv_now + surr * total
                la_next = rho * la_now - beta * surr * total
                lv_now, la_now = lv_next, la_next
            lv_out[:, cols] = lv_now
            la_out[:, cols] = la_now


def stage_contrib(block_index, pieces, weights, stage, n_pos, rec, scan_args, steps):
    rows, local = pieces[0].shape
    _, _, local_blocks, nnz, side, _ = weights.shape
    batch = rows // steps
    n_rounds = len(stage)
    final = scan_args is not None
    has_rec = rec is not None
    operands = list(pieces) + [weights]
    scratch = [
        pltpu.VMEM((len(pieces), rows, local), pieces[0].dtype),
        pltpu.VMEM((n_rounds, local_blocks, nnz, side, side), weights.dtype),
    ]
    n_sem = len(pieces) + n_rounds + (1 if has_rec else 0) + (7 if final else 0)
    scratch.append(pltpu.SemaphoreType.DMA((n_sem,)))
    scratch.append(pltpu.VMEM((steps, batch, local), jnp.float32))
    if has_rec:
        operands.append(rec)
    if final:
        err_grad, surrogate, lv_end, la_end, alpha, rho, beta = scan_args
        rows = [a.reshape(1, local) for a in (alpha, rho, beta)]
        extra = [err_grad, surrogate, lv_end, la_end] + rows
        operands += extra
        scratch += [pltpu.VMEM(a.shape, a.dtype) for a in extra]
        out_specs = (VMEM, VMEM, VMEM)
        out_shape = (
            jax.ShapeDtypeStruct((steps, batch, local), jnp.bfloat16),
            jax.ShapeDtypeStruct((batch, local), jnp.float32),
            jax.ShapeDtypeStruct((batch, local), jnp.float32),
        )
    else:
        out_specs = VMEM
        out_shape = jax.ShapeDtypeStruct((steps, batch, local), jnp.float32)
    kernel = functools.partial(
        stage_kernel, n_pieces=len(pieces), stage=tuple(stage), n_pos=n_pos,
        final=final, has_rec=has_rec,
    )
    pinned = [final and i > len(pieces) + has_rec for i in range(len(operands))]
    specs = [VMEM if p else ANY for p in pinned]
    operands = [pltpu.with_memory_space_constraint(x, pltpu.VMEM) if p else x
                for x, p in zip(operands, pinned)]
    return pl.pallas_call(
        kernel,
        in_specs=[SMEM] + specs,
        out_specs=out_specs,
        scratch_shapes=scratch,
        out_shape=out_shape,
    )(block_index, *operands)


def per_device(
    window, err_grad, surrogate, lv_end, la_end, alpha, rho, beta, weights, block_index, delays
):
    steps = err_grad.shape[0]
    local_neurons = err_grad.shape[2]
    block_side = weights.shape[-1]
    local_blocks = local_neurons // block_side
    rounds = weights.shape[0]
    levels = lax.axis_size("area").bit_length() - 1
    nbits = lax.axis_size("neuron").bit_length() - 1
    n_pos = 1 << nbits
    stages = [list(range(f, min(f + 2, rounds))) for f in range(0, rounds, 2)]
    arrived = []
    gate = None
    for stage in stages:
        pieces = send_slices(window, delays, stage, levels, steps)
        if gate is not None:
            pieces, _ = lax.optimization_barrier((pieces, gate))
        got = [swap(piece, "area", 1 << (rnd % levels)) for piece, rnd in zip(pieces, stage)]
        arrived += got
        gate = got
    groups = stages[:-1] + [[rnd] for rnd in stages[-1]]
    rec = None
    for si, stage in enumerate(groups):
        chunks = []
        for rnd in stage:
            chunks += gather_neuron(arrived[rnd], rec)
        scan_args = None
        if si == len(groups) - 1:
            scan_args = (err_grad, surrogate, lv_end, la_end, alpha, rho, beta)
        rec = stage_contrib(block_index, chunks, weights, stage, n_pos, rec, scan_args, steps)
    return rec


def solution(mesh):
    placed = (
        P(None, "groups", ("area", "neuron")),
        P(None, "groups", ("area", "neuron")),
        P(None, "groups", ("area", "neuron")),
        P("groups", ("area", "neuron")),
        P("groups", ("area", "neuron")),
        P(("area", "neuron")),
        P(("area", "neuron")),
        P(("area", "neuron")),
        P(None, "area", "neuron", None, None, None),
        P(None, "area", "neuron", None),
        P(),
    )
    return jax.shard_map(
        per_device,
        mesh=mesh,
        in_specs=placed,
        out_specs=(
            P(None, "groups", ("area", "neuron")),
            P("groups", ("area", "neuron")),
            P("groups", ("area", "neuron")),
        ),
        check_vma=False,
    )
```

```python
import functools

import jax
import jax.numpy as jnp
from jax import lax
from jax.experimental import pallas as pl
from jax.experimental.pallas import tpu as pltpu
from jax.sharding import PartitionSpec as P

ANY = pl.BlockSpec(memory_space=pl.ANY)
SMEM = pl.BlockSpec(memory_space=pltpu.SMEM)
VMEM = pl.BlockSpec(memory_space=pltpu.VMEM)


def swap(value, axis, mask):
    pairs = [(source, source ^ mask) for source in range(lax.axis_size(axis))]
    return lax.ppermute(value, axis, pairs)


def slice_kernel(delays_ref, window_ref, *outs, rounds, levels, steps):
    me = lax.axis_index("area")
    rows, width = outs[0].shape
    side = 128 if width % 128 == 0 else width
    for rnd, out in zip(rounds, outs):
        start = delays_ref[rnd, me ^ (1 << (rnd % levels))] - steps
        for c in range(0, width, side):
            x = window_ref[pl.ds(start, steps), :, c:c + side].astype(jnp.float32)
            out[:, c:c + side] = x.reshape(rows, side).astype(out.dtype)


def send_slices(window, delays, rounds, levels, steps):
    shape = (steps * window.shape[1], window.shape[2])
    kernel = functools.partial(slice_kernel, rounds=tuple(rounds), levels=levels, steps=steps)
    return pl.pallas_call(
        kernel,
        in_specs=[SMEM, VMEM],
        out_specs=[VMEM] * len(rounds),
        out_shape=[jax.ShapeDtypeStruct(shape, window.dtype)] * len(rounds),
    )(delays, window)


def gather_neuron(held, gate=None, skip=0):
    bits = lax.axis_size("neuron").bit_length() - 1
    held = list(held)
    for bit in list(reversed(range(bits)))[skip:]:
        if bit == 0 and gate is not None:
            held, _ = lax.optimization_barrier((held, gate))
        held = held + [swap(chunk, "neuron", 1 << bit) for chunk in held]
    return held


def swap_diagonal(value, mask, high):
    n_area, n_neuron = lax.axis_size("area"), lax.axis_size("neuron")
    pairs = [
        (a * n_neuron + n, (a ^ mask) * n_neuron + (n ^ high))
        for a in range(n_area)
        for n in range(n_neuron)
    ]
    return lax.ppermute(value, ("area", "neuron"), pairs)


def stage_kernel(bi_ref, *refs, n_pieces, stage, n_pos, final, has_rec):
    n_rounds = len(stage)
    it = iter(refs)
    piece_hbm = [next(it) for _ in range(n_pieces)]
    w_hbm = next(it)
    rec_hbm = next(it) if has_rec else None
    if final:
        scan_hbm = [next(it) for _ in range(7)]
        cur_ref, lv_out, la_out = next(it), next(it), next(it)
    else:
        out_ref = next(it)
    piece_buf = next(it)
    w_buf = next(it)
    sem = next(it)
    rec_buf = next(it)
    if final:
        scan_buf = [next(it) for _ in range(7)]

    steps, batch = rec_buf.shape[0], rec_buf.shape[1]
    local_blocks, nnz, side = w_buf.shape[1], w_buf.shape[2], w_buf.shape[3]
    rows = steps * batch
    bits = n_pos.bit_length() - 1
    me = lax.axis_index("neuron")
    n_sem = 0

    def start(src, dst):
        nonlocal n_sem
        copy = pltpu.make_async_copy(src, dst, sem.at[n_sem])
        n_sem += 1
        copy.start()
        return copy

    piece_cp, w_cp = [], []
    rec_cp = None
    scan_cp = []
    for ri, rnd in enumerate(stage):
        piece_cp += [start(piece_hbm[ri * n_pos + p], piece_buf.at[ri * n_pos + p]) for p in range(n_pos)]
        w_cp.append(start(w_hbm.at[rnd, 0], w_buf.at[ri]))
        if ri == 0 and has_rec:
            rec_cp = start(rec_hbm, rec_buf)
    if final:
        scan_cp = [start(src, dst) for src, dst in zip(scan_hbm, scan_buf)]

    for ri, rnd in enumerate(stage):
        for p in range(n_pos):
            piece_cp[ri * n_pos + p].wait()
        w_cp[ri].wait()
        if ri == 0 and has_rec:
            rec_cp.wait()
        last = ri == n_rounds - 1
        if last and final:
            for copy in scan_cp:
                copy.wait()
            err_buf, surr_buf, lv_buf, la_buf, alpha_buf, rho_buf, beta_buf = scan_buf
        for j in range(local_blocks):
            cols = slice(j * side, (j + 1) * side)
            if ri == 0 and not has_rec:
                acc = jnp.zeros((rows, side), jnp.float32)
            else:
                acc = rec_buf[:, :, cols].reshape(rows, side)
            for k in range(nnz):
                idx = bi_ref[rnd, 0, j, k]
                d = (idx // local_blocks) ^ me
                rel = 0
                for s_, bit in enumerate(reversed(range(bits))):
                    rel = rel | (((d >> bit) & 1) << s_)
                off = pl.multiple_of((idx % local_blocks) * side, side)
                x = piece_buf[ri * n_pos + rel, :, pl.ds(off, side)]
                acc = acc + jnp.dot(x, w_buf[ri, j, k], preferred_element_type=jnp.float32)
            rec = acc.reshape(steps, batch, side)
            if not last:
                rec_buf[:, :, cols] = rec
                continue
            if not final:
                out_ref[:, :, cols] = rec
                continue
            alpha = alpha_buf[:, cols]
            rho = rho_buf[:, cols]
            beta = beta_buf[:, cols]
            lv_now = lv_buf[:, cols]
            la_now = la_buf[:, cols]
            for t in reversed(range(steps)):
                surr = surr_buf[t, :, cols]
                total = err_buf[t, :, cols] + rec[t] - lv_now + la_now
                cur_ref[t, :, cols] = lv_now.astype(cur_ref.dtype)
                lv_next = alpha * lv_now + surr * total
                la_next = rho * la_now - beta * surr * total
                lv_now, la_now = lv_next, la_next
            lv_out[:, cols] = lv_now
            la_out[:, cols] = la_now


def stage_contrib(block_index, pieces, weights, stage, n_pos, rec, scan_args, steps):
    rows, local = pieces[0].shape
    _, _, local_blocks, nnz, side, _ = weights.shape
    batch = rows // steps
    n_rounds = len(stage)
    final = scan_args is not None
    has_rec = rec is not None
    operands = list(pieces) + [weights]
    scratch = [
        pltpu.VMEM((len(pieces), rows, local), pieces[0].dtype),
        pltpu.VMEM((n_rounds, local_blocks, nnz, side, side), weights.dtype),
    ]
    n_sem = len(pieces) + n_rounds + (1 if has_rec else 0) + (7 if final else 0)
    scratch.append(pltpu.SemaphoreType.DMA((n_sem,)))
    scratch.append(pltpu.VMEM((steps, batch, local), jnp.float32))
    if has_rec:
        operands.append(rec)
    if final:
        err_grad, surrogate, lv_end, la_end, alpha, rho, beta = scan_args
        rows = [a.reshape(1, local) for a in (alpha, rho, beta)]
        extra = [err_grad, surrogate, lv_end, la_end] + rows
        operands += extra
        scratch += [pltpu.VMEM(a.shape, a.dtype) for a in extra]
        out_specs = (VMEM, VMEM, VMEM)
        out_shape = (
            jax.ShapeDtypeStruct((steps, batch, local), jnp.bfloat16),
            jax.ShapeDtypeStruct((batch, local), jnp.float32),
            jax.ShapeDtypeStruct((batch, local), jnp.float32),
        )
    else:
        out_specs = VMEM
        out_shape = jax.ShapeDtypeStruct((steps, batch, local), jnp.float32)
    kernel = functools.partial(
        stage_kernel, n_pieces=len(pieces), stage=tuple(stage), n_pos=n_pos,
        final=final, has_rec=has_rec,
    )
    pinned = [final and i > len(pieces) + has_rec for i in range(len(operands))]
    specs = [VMEM if p else ANY for p in pinned]
    operands = [pltpu.with_memory_space_constraint(x, pltpu.VMEM) if p else x
                for x, p in zip(operands, pinned)]
    return pl.pallas_call(
        kernel,
        in_specs=[SMEM] + specs,
        out_specs=out_specs,
        scratch_shapes=scratch,
        out_shape=out_shape,
    )(block_index, *operands)


def per_device(
    window, err_grad, surrogate, lv_end, la_end, alpha, rho, beta, weights, block_index, delays
):
    steps = err_grad.shape[0]
    local_neurons = err_grad.shape[2]
    block_side = weights.shape[-1]
    local_blocks = local_neurons // block_side
    rounds = weights.shape[0]
    levels = lax.axis_size("area").bit_length() - 1
    nbits = lax.axis_size("neuron").bit_length() - 1
    n_pos = 1 << nbits
    stages = [list(range(f, min(f + 2, rounds))) for f in range(0, rounds, 2)]
    high = (1 << (nbits - 1)) if nbits > 0 else 0
    arrived = {}
    gate = None
    for si, stage in enumerate(stages):
        pieces = send_slices(window, delays, stage, levels, steps)
        if gate is not None:
            pieces, _ = lax.optimization_barrier((pieces, gate))
        diagonal = si == len(stages) - 1 and si > 0 and high > 0
        got = []
        for piece, rnd in zip(pieces, stage):
            mask = 1 << (rnd % levels)
            straight = swap(piece, "area", mask)
            arrived[rnd] = [straight, swap_diagonal(piece, mask, high)] if diagonal else [straight]
            got.append(straight)
        gate = got
    rec = None
    for si, stage in enumerate(stages):
        chunks = []
        for rnd in stage:
            chunks += gather_neuron(arrived[rnd], rec, len(arrived[rnd]) - 1)
        scan_args = None
        if si == len(stages) - 1:
            scan_args = (err_grad, surrogate, lv_end, la_end, alpha, rho, beta)
        rec = stage_contrib(block_index, chunks, weights, stage, n_pos, rec, scan_args, steps)
    return rec


def solution(mesh):
    placed = (
        P(None, "groups", ("area", "neuron")),
        P(None, "groups", ("area", "neuron")),
        P(None, "groups", ("area", "neuron")),
        P("groups", ("area", "neuron")),
        P("groups", ("area", "neuron")),
        P(("area", "neuron")),
        P(("area", "neuron")),
        P(("area", "neuron")),
        P(None, "area", "neuron", None, None, None),
        P(None, "area", "neuron", None),
        P(),
    )
    return jax.shard_map(
        per_device,
        mesh=mesh,
        in_specs=placed,
        out_specs=(
            P(None, "groups", ("area", "neuron")),
            P("groups", ("area", "neuron")),
            P("groups", ("area", "neuron")),
        ),
        check_vma=False,
    )
```

```python
import functools

import jax
import jax.numpy as jnp
from jax import lax
from jax.experimental import pallas as pl
from jax.experimental.pallas import tpu as pltpu
from jax.sharding import PartitionSpec as P

ANY = pl.BlockSpec(memory_space=pl.ANY)
SMEM = pl.BlockSpec(memory_space=pltpu.SMEM)
VMEM = pl.BlockSpec(memory_space=pltpu.VMEM)


def swap(value, axis, mask):
    pairs = [(source, source ^ mask) for source in range(lax.axis_size(axis))]
    return lax.ppermute(value, axis, pairs)


def slice_kernel(delays_ref, window_ref, *outs, rounds, levels, steps):
    me = lax.axis_index("area")
    rows, width = outs[0].shape
    side = 128 if width % 128 == 0 else width
    for rnd, out in zip(rounds, outs):
        start = delays_ref[rnd, me ^ (1 << (rnd % levels))] - steps
        for c in range(0, width, side):
            x = window_ref[pl.ds(start, steps), :, c:c + side].astype(jnp.float32)
            out[:, c:c + side] = x.reshape(rows, side).astype(out.dtype)


def send_slices(window, delays, rounds, levels, steps):
    shape = (steps * window.shape[1], window.shape[2])
    kernel = functools.partial(slice_kernel, rounds=tuple(rounds), levels=levels, steps=steps)
    return pl.pallas_call(
        kernel,
        in_specs=[SMEM, VMEM],
        out_specs=[VMEM] * len(rounds),
        out_shape=[jax.ShapeDtypeStruct(shape, window.dtype)] * len(rounds),
    )(delays, window)


def gather_neuron(piece, gate=None):
    bits = lax.axis_size("neuron").bit_length() - 1
    held = [piece]
    for bit in reversed(range(bits)):
        if bit == 0 and gate is not None:
            held, _ = lax.optimization_barrier((held, gate))
        held = held + [swap(chunk, "neuron", 1 << bit) for chunk in held]
    return held


def stage_kernel(bi_ref, *refs, n_pieces, stage, n_pos, final, has_rec):
    n_rounds = len(stage)
    it = iter(refs)
    piece_hbm = [next(it) for _ in range(n_pieces)]
    w_hbm = next(it)
    rec_hbm = next(it) if has_rec else None
    if final:
        scan_hbm = [next(it) for _ in range(7)]
        cur_ref, lv_out, la_out = next(it), next(it), next(it)
    else:
        out_ref = next(it)
    piece_buf = next(it)
    w_buf = next(it)
    sem = next(it)
    rec_buf = next(it)
    if final:
        scan_buf = [next(it) for _ in range(7)]

    steps, batch = rec_buf.shape[0], rec_buf.shape[1]
    local_blocks, nnz, side = w_buf.shape[1], w_buf.shape[2], w_buf.shape[3]
    rows = steps * batch
    bits = n_pos.bit_length() - 1
    me = lax.axis_index("neuron")
    n_sem = 0

    def start(src, dst):
        nonlocal n_sem
        copy = pltpu.make_async_copy(src, dst, sem.at[n_sem])
        n_sem += 1
        copy.start()
        return copy

    piece_cp, w_cp = [], []
    rec_cp = None
    scan_cp = []
    for ri, rnd in enumerate(stage):
        piece_cp += [start(piece_hbm[ri * n_pos + p], piece_buf.at[ri * n_pos + p]) for p in range(n_pos)]
        w_cp.append(start(w_hbm.at[rnd, 0], w_buf.at[ri]))
        if ri == 0 and has_rec:
            rec_cp = start(rec_hbm, rec_buf)
    if final:
        scan_cp = [start(src, dst) for src, dst in zip(scan_hbm, scan_buf)]

    for ri, rnd in enumerate(stage):
        for p in range(n_pos):
            piece_cp[ri * n_pos + p].wait()
        w_cp[ri].wait()
        if ri == 0 and has_rec:
            rec_cp.wait()
        last = ri == n_rounds - 1
        if last and final:
            for copy in scan_cp:
                copy.wait()
            err_buf, surr_buf, lv_buf, la_buf, alpha_buf, rho_buf, beta_buf = scan_buf
        for j in range(local_blocks):
            cols = slice(j * side, (j + 1) * side)
            if ri == 0 and not has_rec:
                acc = jnp.zeros((rows, side), jnp.float32)
            else:
                acc = rec_buf[:, :, cols].reshape(rows, side)
            for k in range(nnz):
                idx = bi_ref[rnd, 0, j, k]
                d = (idx // local_blocks) ^ me
                rel = 0
                for s_, bit in enumerate(reversed(range(bits))):
                    rel = rel | (((d >> bit) & 1) << s_)
                off = pl.multiple_of((idx % local_blocks) * side, side)
                x = piece_buf[ri * n_pos + rel, :, pl.ds(off, side)]
                acc = acc + jnp.dot(x, w_buf[ri, j, k], preferred_element_type=jnp.float32)
            rec = acc.reshape(steps, batch, side)
            if not last:
                rec_buf[:, :, cols] = rec
                continue
            if not final:
                out_ref[:, :, cols] = rec
                continue
            alpha = alpha_buf[:, cols]
            rho = rho_buf[:, cols]
            beta = beta_buf[:, cols]
            lv_now = lv_buf[:, cols]
            la_now = la_buf[:, cols]
            for t in reversed(range(steps)):
                surr = surr_buf[t, :, cols]
                total = err_buf[t, :, cols] + rec[t] - lv_now + la_now
                cur_ref[t, :, cols] = lv_now.astype(cur_ref.dtype)
                lv_next = alpha * lv_now + surr * total
                la_next = rho * la_now - beta * surr * total
                lv_now, la_now = lv_next, la_next
            lv_out[:, cols] = lv_now
            la_out[:, cols] = la_now


def stage_contrib(block_index, pieces, weights, stage, n_pos, rec, scan_args, steps):
    rows, local = pieces[0].shape
    _, _, local_blocks, nnz, side, _ = weights.shape
    batch = rows // steps
    n_rounds = len(stage)
    final = scan_args is not None
    has_rec = rec is not None
    operands = list(pieces) + [weights]
    scratch = [
        pltpu.VMEM((len(pieces), rows, local), pieces[0].dtype),
        pltpu.VMEM((n_rounds, local_blocks, nnz, side, side), weights.dtype),
    ]
    n_sem = len(pieces) + n_rounds + (1 if has_rec else 0) + (7 if final else 0)
    scratch.append(pltpu.SemaphoreType.DMA((n_sem,)))
    scratch.append(pltpu.VMEM((steps, batch, local), jnp.float32))
    if has_rec:
        operands.append(rec)
    if final:
        err_grad, surrogate, lv_end, la_end, alpha, rho, beta = scan_args
        rows = [a.reshape(1, local) for a in (alpha, rho, beta)]
        extra = [err_grad, surrogate, lv_end, la_end] + rows
        operands += extra
        scratch += [pltpu.VMEM(a.shape, a.dtype) for a in extra]
        out_specs = (VMEM, VMEM, VMEM)
        out_shape = (
            jax.ShapeDtypeStruct((steps, batch, local), jnp.bfloat16),
            jax.ShapeDtypeStruct((batch, local), jnp.float32),
            jax.ShapeDtypeStruct((batch, local), jnp.float32),
        )
    else:
        out_specs = VMEM
        out_shape = jax.ShapeDtypeStruct((steps, batch, local), jnp.float32)
    kernel = functools.partial(
        stage_kernel, n_pieces=len(pieces), stage=tuple(stage), n_pos=n_pos,
        final=final, has_rec=has_rec,
    )
    pinned = [final and i > len(pieces) + has_rec for i in range(len(operands))]
    specs = [VMEM if p else ANY for p in pinned]
    operands = [pltpu.with_memory_space_constraint(x, pltpu.VMEM) if p else x
                for x, p in zip(operands, pinned)]
    return pl.pallas_call(
        kernel,
        in_specs=[SMEM] + specs,
        out_specs=out_specs,
        scratch_shapes=scratch,
        out_shape=out_shape,
    )(block_index, *operands)


def per_device(
    window, err_grad, surrogate, lv_end, la_end, alpha, rho, beta, weights, block_index, delays
):
    steps = err_grad.shape[0]
    local_neurons = err_grad.shape[2]
    block_side = weights.shape[-1]
    local_blocks = local_neurons // block_side
    rounds = weights.shape[0]
    levels = lax.axis_size("area").bit_length() - 1
    nbits = lax.axis_size("neuron").bit_length() - 1
    n_pos = 1 << nbits
    stages = [list(range(f, min(f + 2, rounds))) for f in range(0, rounds, 2)]
    arrived = {}
    gate = None
    for stage in stages:
        stage = sorted(stage, key=lambda rnd: -(rnd % levels))
        pieces = send_slices(window, delays, stage, levels, steps)
        if gate is not None:
            pieces, _ = lax.optimization_barrier((pieces, gate))
        got = [swap(piece, "area", 1 << (rnd % levels)) for piece, rnd in zip(pieces, stage)]
        arrived.update(zip(stage, got))
        gate = got
    rec = None
    for si, stage in enumerate(stages):
        chunks = []
        for rnd in stage:
            chunks += gather_neuron(arrived[rnd], rec)
        scan_args = None
        if si == len(stages) - 1:
            scan_args = (err_grad, surrogate, lv_end, la_end, alpha, rho, beta)
        rec = stage_contrib(block_index, chunks, weights, stage, n_pos, rec, scan_args, steps)
    return rec


def solution(mesh):
    placed = (
        P(None, "groups", ("area", "neuron")),
        P(None, "groups", ("area", "neuron")),
        P(None, "groups", ("area", "neuron")),
        P("groups", ("area", "neuron")),
        P("groups", ("area", "neuron")),
        P(("area", "neuron")),
        P(("area", "neuron")),
        P(("area", "neuron")),
        P(None, "area", "neuron", None, None, None),
        P(None, "area", "neuron", None),
        P(),
    )
    return jax.shard_map(
        per_device,
        mesh=mesh,
        in_specs=placed,
        out_specs=(
            P(None, "groups", ("area", "neuron")),
            P("groups", ("area", "neuron")),
            P("groups", ("area", "neuron")),
        ),
        check_vma=False,
    )
```

```python
import functools

import jax
import jax.numpy as jnp
from jax import lax
from jax.experimental import pallas as pl
from jax.experimental.pallas import tpu as pltpu
from jax.sharding import PartitionSpec as P

ANY = pl.BlockSpec(memory_space=pl.ANY)
SMEM = pl.BlockSpec(memory_space=pltpu.SMEM)
VMEM = pl.BlockSpec(memory_space=pltpu.VMEM)


def swap(value, axis, mask):
    pairs = [(source, source ^ mask) for source in range(lax.axis_size(axis))]
    return lax.ppermute(value, axis, pairs)


def slice_kernel(delays_ref, window_ref, *outs, rounds, levels, steps, n_halves):
    me = lax.axis_index("area")
    rows, width = outs[0].shape
    side = 128 if width % 128 == 0 else width
    for n, out in enumerate(outs):
        rnd, h = rounds[n // n_halves], n % n_halves
        start = delays_ref[rnd, me ^ (1 << (rnd % levels))] - steps
        for c in range(0, width, side):
            col = h * width + c
            x = window_ref[pl.ds(start, steps), :, col:col + side].astype(jnp.float32)
            out[:, c:c + side] = x.reshape(rows, side).astype(out.dtype)


def send_slices(window, delays, rounds, levels, steps, n_halves=1):
    shape = (steps * window.shape[1], window.shape[2] // n_halves)
    kernel = functools.partial(
        slice_kernel, rounds=tuple(rounds), levels=levels, steps=steps, n_halves=n_halves
    )
    n_out = len(rounds) * n_halves
    return pl.pallas_call(
        kernel,
        in_specs=[SMEM, VMEM],
        out_specs=[VMEM] * n_out,
        out_shape=[jax.ShapeDtypeStruct(shape, window.dtype)] * n_out,
    )(delays, window)


def gather_neuron(piece, gate=None):
    bits = lax.axis_size("neuron").bit_length() - 1
    held = [piece]
    for bit in reversed(range(bits)):
        if bit == 0 and gate is not None:
            held, _ = lax.optimization_barrier((held, gate))
        held = held + [swap(chunk, "neuron", 1 << bit) for chunk in held]
    return held


def stage_kernel(bi_ref, *refs, n_pieces, stage, n_pos, n_halves, final, has_rec):
    n_rounds = len(stage)
    it = iter(refs)
    piece_hbm = [next(it) for _ in range(n_pieces)]
    w_hbm = next(it)
    rec_hbm = next(it) if has_rec else None
    if final:
        scan_hbm = [next(it) for _ in range(7)]
        cur_ref, lv_out, la_out = next(it), next(it), next(it)
    else:
        out_ref = next(it)
    piece_buf = next(it)
    w_buf = next(it)
    sem = next(it)
    rec_buf = next(it)
    if final:
        scan_buf = [next(it) for _ in range(7)]

    steps, batch = rec_buf.shape[0], rec_buf.shape[1]
    local_blocks, nnz, side = w_buf.shape[1], w_buf.shape[2], w_buf.shape[3]
    rows = steps * batch
    bits = n_pos.bit_length() - 1
    me = lax.axis_index("neuron")
    n_sem = 0

    def start(src, dst):
        nonlocal n_sem
        copy = pltpu.make_async_copy(src, dst, sem.at[n_sem])
        n_sem += 1
        copy.start()
        return copy

    piece_cp, w_cp = [], []
    rec_cp = None
    scan_cp = []
    width = piece_buf.shape[-1] // n_halves
    for ri, rnd in enumerate(stage):
        for p in range(n_pos):
            for h in range(n_halves):
                dst = piece_buf.at[ri * n_pos + p, :, pl.ds(h * width, width)]
                piece_cp.append(start(piece_hbm[(ri * n_pos + p) * n_halves + h], dst))
        w_cp.append(start(w_hbm.at[rnd, 0], w_buf.at[ri]))
        if ri == 0 and has_rec:
            rec_cp = start(rec_hbm, rec_buf)
    if final:
        scan_cp = [start(src, dst) for src, dst in zip(scan_hbm, scan_buf)]

    for ri, rnd in enumerate(stage):
        for q in range(n_pos * n_halves):
            piece_cp[ri * n_pos * n_halves + q].wait()
        w_cp[ri].wait()
        if ri == 0 and has_rec:
            rec_cp.wait()
        last = ri == n_rounds - 1
        if last and final:
            for copy in scan_cp:
                copy.wait()
            err_buf, surr_buf, lv_buf, la_buf, alpha_buf, rho_buf, beta_buf = scan_buf
        for j in range(local_blocks):
            cols = slice(j * side, (j + 1) * side)
            if ri == 0 and not has_rec:
                acc = jnp.zeros((rows, side), jnp.float32)
            else:
                acc = rec_buf[:, :, cols].reshape(rows, side)
            for k in range(nnz):
                idx = bi_ref[rnd, 0, j, k]
                d = (idx // local_blocks) ^ me
                rel = 0
                for s_, bit in enumerate(reversed(range(bits))):
                    rel = rel | (((d >> bit) & 1) << s_)
                off = pl.multiple_of((idx % local_blocks) * side, side)
                x = piece_buf[ri * n_pos + rel, :, pl.ds(off, side)]
                acc = acc + jnp.dot(x, w_buf[ri, j, k], preferred_element_type=jnp.float32)
            rec = acc.reshape(steps, batch, side)
            if not last:
                rec_buf[:, :, cols] = rec
                continue
            if not final:
                out_ref[:, :, cols] = rec
                continue
            alpha = alpha_buf[:, cols]
            rho = rho_buf[:, cols]
            beta = beta_buf[:, cols]
            lv_now = lv_buf[:, cols]
            la_now = la_buf[:, cols]
            for t in reversed(range(steps)):
                surr = surr_buf[t, :, cols]
                total = err_buf[t, :, cols] + rec[t] - lv_now + la_now
                cur_ref[t, :, cols] = lv_now.astype(cur_ref.dtype)
                lv_next = alpha * lv_now + surr * total
                la_next = rho * la_now - beta * surr * total
                lv_now, la_now = lv_next, la_next
            lv_out[:, cols] = lv_now
            la_out[:, cols] = la_now


def stage_contrib(block_index, pieces, weights, stage, n_pos, rec, scan_args, steps, n_halves=1):
    rows, width = pieces[0].shape
    local = width * n_halves
    _, _, local_blocks, nnz, side, _ = weights.shape
    batch = rows // steps
    n_rounds = len(stage)
    final = scan_args is not None
    has_rec = rec is not None
    operands = list(pieces) + [weights]
    scratch = [
        pltpu.VMEM((len(pieces) // n_halves, rows, local), pieces[0].dtype),
        pltpu.VMEM((n_rounds, local_blocks, nnz, side, side), weights.dtype),
    ]
    n_sem = len(pieces) + n_rounds + (1 if has_rec else 0) + (7 if final else 0)
    scratch.append(pltpu.SemaphoreType.DMA((n_sem,)))
    scratch.append(pltpu.VMEM((steps, batch, local), jnp.float32))
    if has_rec:
        operands.append(rec)
    if final:
        err_grad, surrogate, lv_end, la_end, alpha, rho, beta = scan_args
        rows = [a.reshape(1, local) for a in (alpha, rho, beta)]
        extra = [err_grad, surrogate, lv_end, la_end] + rows
        operands += extra
        scratch += [pltpu.VMEM(a.shape, a.dtype) for a in extra]
        out_specs = (VMEM, VMEM, VMEM)
        out_shape = (
            jax.ShapeDtypeStruct((steps, batch, local), jnp.bfloat16),
            jax.ShapeDtypeStruct((batch, local), jnp.float32),
            jax.ShapeDtypeStruct((batch, local), jnp.float32),
        )
    else:
        out_specs = VMEM
        out_shape = jax.ShapeDtypeStruct((steps, batch, local), jnp.float32)
    kernel = functools.partial(
        stage_kernel, n_pieces=len(pieces), stage=tuple(stage), n_pos=n_pos, n_halves=n_halves,
        final=final, has_rec=has_rec,
    )
    pinned = [final and i > len(pieces) + has_rec for i in range(len(operands))]
    specs = [VMEM if p else ANY for p in pinned]
    operands = [pltpu.with_memory_space_constraint(x, pltpu.VMEM) if p else x
                for x, p in zip(operands, pinned)]
    return pl.pallas_call(
        kernel,
        in_specs=[SMEM] + specs,
        out_specs=out_specs,
        scratch_shapes=scratch,
        out_shape=out_shape,
    )(block_index, *operands)


def per_device(
    window, err_grad, surrogate, lv_end, la_end, alpha, rho, beta, weights, block_index, delays
):
    steps = err_grad.shape[0]
    local_neurons = err_grad.shape[2]
    block_side = weights.shape[-1]
    local_blocks = local_neurons // block_side
    rounds = weights.shape[0]
    levels = lax.axis_size("area").bit_length() - 1
    nbits = lax.axis_size("neuron").bit_length() - 1
    n_pos = 1 << nbits
    stages = [list(range(f, min(f + 2, rounds))) for f in range(0, rounds, 2)]
    n_halves = 2 if local_blocks % 2 == 0 and len(stages) > 1 else 1
    arrived = {}
    gate = None
    for si, stage in enumerate(stages):
        halves = n_halves if si == len(stages) - 1 else 1
        pieces = send_slices(window, delays, stage, levels, steps, halves)
        for h in range(halves):
            part = [pieces[ri * halves + h] for ri in range(len(stage))]
            if gate is not None:
                part, _ = lax.optimization_barrier((part, gate))
            got = [swap(piece, "area", 1 << (rnd % levels)) for piece, rnd in zip(part, stage)]
            for rnd, g in zip(stage, got):
                arrived[(rnd, h)] = g
            gate = got
    rec = None
    for si, stage in enumerate(stages):
        halves = n_halves if si == len(stages) - 1 else 1
        chunks = []
        for rnd in stage:
            parts = [gather_neuron(arrived[(rnd, h)], rec) for h in range(halves)]
            chunks += [parts[h][p] for p in range(n_pos) for h in range(halves)]
        scan_args = None
        if si == len(stages) - 1:
            scan_args = (err_grad, surrogate, lv_end, la_end, alpha, rho, beta)
        rec = stage_contrib(
            block_index, chunks, weights, stage, n_pos, rec, scan_args, steps, halves
        )
    return rec


def solution(mesh):
    placed = (
        P(None, "groups", ("area", "neuron")),
        P(None, "groups", ("area", "neuron")),
        P(None, "groups", ("area", "neuron")),
        P("groups", ("area", "neuron")),
        P("groups", ("area", "neuron")),
        P(("area", "neuron")),
        P(("area", "neuron")),
        P(("area", "neuron")),
        P(None, "area", "neuron", None, None, None),
        P(None, "area", "neuron", None),
        P(),
    )
    return jax.shard_map(
        per_device,
        mesh=mesh,
        in_specs=placed,
        out_specs=(
            P(None, "groups", ("area", "neuron")),
            P("groups", ("area", "neuron")),
            P("groups", ("area", "neuron")),
        ),
        check_vma=False,
    )
```

```python
import functools

import jax
import jax.numpy as jnp
from jax import lax
from jax.experimental import pallas as pl
from jax.experimental.pallas import tpu as pltpu
from jax.sharding import PartitionSpec as P

ANY = pl.BlockSpec(memory_space=pl.ANY)
SMEM = pl.BlockSpec(memory_space=pltpu.SMEM)
VMEM = pl.BlockSpec(memory_space=pltpu.VMEM)


def swap(value, axis, mask):
    pairs = [(source, source ^ mask) for source in range(lax.axis_size(axis))]
    return lax.ppermute(value, axis, pairs)


def slice_kernel(delays_ref, window_ref, *outs, rounds, levels, steps):
    me = lax.axis_index("area")
    rows, width = outs[0].shape
    side = 128 if width % 128 == 0 else width
    for rnd, out in zip(rounds, outs):
        start = delays_ref[rnd, me ^ (1 << (rnd % levels))] - steps
        for c in range(0, width, side):
            x = window_ref[pl.ds(start, steps), :, c:c + side].astype(jnp.float32)
            out[:, c:c + side] = x.reshape(rows, side).astype(out.dtype)


def send_slices(window, delays, rounds, levels, steps):
    shape = (steps * window.shape[1], window.shape[2])
    kernel = functools.partial(slice_kernel, rounds=tuple(rounds), levels=levels, steps=steps)
    return pl.pallas_call(
        kernel,
        in_specs=[SMEM, VMEM],
        out_specs=[VMEM] * len(rounds),
        out_shape=[jax.ShapeDtypeStruct(shape, window.dtype)] * len(rounds),
    )(delays, window)


def gather_neuron(piece, gate=None):
    bits = lax.axis_size("neuron").bit_length() - 1
    held = [piece]
    for bit in reversed(range(bits)):
        if bit == 0 and gate is not None:
            held, _ = lax.optimization_barrier((held, gate))
        held = held + [swap(chunk, "neuron", 1 << bit) for chunk in held]
    return held


def stage_kernel(bi_ref, *refs, n_pieces, stage, n_pos, final, has_rec):
    n_rounds = len(stage)
    it = iter(refs)
    piece_hbm = [next(it) for _ in range(n_pieces)]
    w_hbm = next(it)
    rec_hbm = next(it) if has_rec else None
    if final:
        scan_hbm = [next(it) for _ in range(7)]
        cur_ref, lv_out, la_out = next(it), next(it), next(it)
    else:
        out_ref = next(it)
    piece_buf = next(it)
    w_buf = next(it)
    sem = next(it)
    rec_buf = next(it)

    steps, batch = rec_buf.shape[0], rec_buf.shape[1]
    local_blocks, nnz, side = w_buf.shape[1], w_buf.shape[2], w_buf.shape[3]
    rows = steps * batch
    bits = n_pos.bit_length() - 1
    me = lax.axis_index("neuron")
    n_sem = 0

    def start(src, dst):
        nonlocal n_sem
        copy = pltpu.make_async_copy(src, dst, sem.at[n_sem])
        n_sem += 1
        copy.start()
        return copy

    piece_cp, w_cp = [], []
    rec_cp = None
    for ri, rnd in enumerate(stage):
        piece_cp += [start(piece_hbm[ri * n_pos + p], piece_buf.at[ri * n_pos + p]) for p in range(n_pos)]
        w_cp.append(start(w_hbm.at[rnd, 0], w_buf.at[ri]))
        if ri == 0 and has_rec:
            rec_cp = start(rec_hbm, rec_buf)

    for ri, rnd in enumerate(stage):
        for p in range(n_pos):
            piece_cp[ri * n_pos + p].wait()
        w_cp[ri].wait()
        if ri == 0 and has_rec:
            rec_cp.wait()
        last = ri == n_rounds - 1
        if last and final:
            err_buf, surr_buf, lv_buf, la_buf, alpha_buf, rho_buf, beta_buf = scan_hbm
        for j in range(local_blocks):
            cols = slice(j * side, (j + 1) * side)
            if ri == 0 and not has_rec:
                acc = jnp.zeros((rows, side), jnp.float32)
            else:
                acc = rec_buf[:, :, cols].reshape(rows, side)
            for k in range(nnz):
                idx = bi_ref[rnd, 0, j, k]
                d = (idx // local_blocks) ^ me
                rel = 0
                for s_, bit in enumerate(reversed(range(bits))):
                    rel = rel | (((d >> bit) & 1) << s_)
                off = pl.multiple_of((idx % local_blocks) * side, side)
                x = piece_buf[ri * n_pos + rel, :, pl.ds(off, side)]
                acc = acc + jnp.dot(x, w_buf[ri, j, k], preferred_element_type=jnp.float32)
            rec = acc.reshape(steps, batch, side)
            if not last:
                rec_buf[:, :, cols] = rec
                continue
            if not final:
                out_ref[:, :, cols] = rec
                continue
            alpha = alpha_buf[:, cols]
            rho = rho_buf[:, cols]
            beta = beta_buf[:, cols]
            lv_now = lv_buf[:, cols]
            la_now = la_buf[:, cols]
            for t in reversed(range(steps)):
                surr = surr_buf[t, :, cols]
                total = err_buf[t, :, cols] + rec[t] - lv_now + la_now
                cur_ref[t, :, cols] = lv_now.astype(cur_ref.dtype)
                lv_next = alpha * lv_now + surr * total
                la_next = rho * la_now - beta * surr * total
                lv_now, la_now = lv_next, la_next
            lv_out[:, cols] = lv_now
            la_out[:, cols] = la_now


def stage_contrib(block_index, pieces, weights, stage, n_pos, rec, scan_args, steps):
    rows, local = pieces[0].shape
    _, _, local_blocks, nnz, side, _ = weights.shape
    batch = rows // steps
    n_rounds = len(stage)
    final = scan_args is not None
    has_rec = rec is not None
    operands = list(pieces) + [weights]
    scratch = [
        pltpu.VMEM((len(pieces), rows, local), pieces[0].dtype),
        pltpu.VMEM((n_rounds, local_blocks, nnz, side, side), weights.dtype),
    ]
    n_sem = len(pieces) + n_rounds + (1 if has_rec else 0)
    scratch.append(pltpu.SemaphoreType.DMA((n_sem,)))
    scratch.append(pltpu.VMEM((steps, batch, local), jnp.float32))
    if has_rec:
        operands.append(rec)
    if final:
        err_grad, surrogate, lv_end, la_end, alpha, rho, beta = scan_args
        rows = [a.reshape(1, local) for a in (alpha, rho, beta)]
        extra = [err_grad, surrogate, lv_end, la_end] + rows
        operands += extra
        out_specs = (VMEM, VMEM, VMEM)
        out_shape = (
            jax.ShapeDtypeStruct((steps, batch, local), jnp.bfloat16),
            jax.ShapeDtypeStruct((batch, local), jnp.float32),
            jax.ShapeDtypeStruct((batch, local), jnp.float32),
        )
    else:
        out_specs = VMEM
        out_shape = jax.ShapeDtypeStruct((steps, batch, local), jnp.float32)
    kernel = functools.partial(
        stage_kernel, n_pieces=len(pieces), stage=tuple(stage), n_pos=n_pos,
        final=final, has_rec=has_rec,
    )
    pinned = [final and i > len(pieces) + has_rec for i in range(len(operands))]
    specs = [VMEM if p else ANY for p in pinned]
    operands = [pltpu.with_memory_space_constraint(x, pltpu.VMEM) if p else x
                for x, p in zip(operands, pinned)]
    return pl.pallas_call(
        kernel,
        in_specs=[SMEM] + specs,
        out_specs=out_specs,
        scratch_shapes=scratch,
        out_shape=out_shape,
    )(block_index, *operands)


def per_device(
    window, err_grad, surrogate, lv_end, la_end, alpha, rho, beta, weights, block_index, delays
):
    steps = err_grad.shape[0]
    local_neurons = err_grad.shape[2]
    block_side = weights.shape[-1]
    local_blocks = local_neurons // block_side
    rounds = weights.shape[0]
    levels = lax.axis_size("area").bit_length() - 1
    nbits = lax.axis_size("neuron").bit_length() - 1
    n_pos = 1 << nbits
    stages = [list(range(f, min(f + 2, rounds))) for f in range(0, rounds, 2)]
    arrived = []
    gate = None
    for stage in stages:
        pieces = send_slices(window, delays, stage, levels, steps)
        if gate is not None:
            pieces, _ = lax.optimization_barrier((pieces, gate))
        got = [swap(piece, "area", 1 << (rnd % levels)) for piece, rnd in zip(pieces, stage)]
        arrived += got
        gate = got
    rec = None
    for si, stage in enumerate(stages):
        chunks = []
        for rnd in stage:
            chunks += gather_neuron(arrived[rnd], rec)
        scan_args = None
        if si == len(stages) - 1:
            scan_args = (err_grad, surrogate, lv_end, la_end, alpha, rho, beta)
        rec = stage_contrib(block_index, chunks, weights, stage, n_pos, rec, scan_args, steps)
    return rec


def solution(mesh):
    placed = (
        P(None, "groups", ("area", "neuron")),
        P(None, "groups", ("area", "neuron")),
        P(None, "groups", ("area", "neuron")),
        P("groups", ("area", "neuron")),
        P("groups", ("area", "neuron")),
        P(("area", "neuron")),
        P(("area", "neuron")),
        P(("area", "neuron")),
        P(None, "area", "neuron", None, None, None),
        P(None, "area", "neuron", None),
        P(),
    )
    return jax.shard_map(
        per_device,
        mesh=mesh,
        in_specs=placed,
        out_specs=(
            P(None, "groups", ("area", "neuron")),
            P("groups", ("area", "neuron")),
            P("groups", ("area", "neuron")),
        ),
        check_vma=False,
    )
```

```python
import functools

import jax
import jax.numpy as jnp
from jax import lax
from jax.experimental import pallas as pl
from jax.experimental.pallas import tpu as pltpu
from jax.sharding import PartitionSpec as P

ANY = pl.BlockSpec(memory_space=pl.ANY)
SMEM = pl.BlockSpec(memory_space=pltpu.SMEM)
VMEM = pl.BlockSpec(memory_space=pltpu.VMEM)


def swap(value, axis, mask):
    pairs = [(source, source ^ mask) for source in range(lax.axis_size(axis))]
    return lax.ppermute(value, axis, pairs)


def slice_kernel(delays_ref, window_ref, *outs, rounds, levels, steps):
    me = lax.axis_index("area")
    rows, width = outs[0].shape
    side = 128 if width % 128 == 0 else width
    for rnd, out in zip(rounds, outs):
        start = delays_ref[rnd, me ^ (1 << (rnd % levels))] - steps
        for c in range(0, width, side):
            x = window_ref[pl.ds(start, steps), :, c:c + side].astype(jnp.float32)
            out[:, c:c + side] = x.reshape(rows, side).astype(out.dtype)


def send_slices(window, delays, rounds, levels, steps):
    shape = (steps * window.shape[1], window.shape[2])
    kernel = functools.partial(slice_kernel, rounds=tuple(rounds), levels=levels, steps=steps)
    return pl.pallas_call(
        kernel,
        in_specs=[SMEM, VMEM],
        out_specs=[VMEM] * len(rounds),
        out_shape=[jax.ShapeDtypeStruct(shape, window.dtype)] * len(rounds),
    )(delays, window)


def gather_neuron(piece, gate=None):
    bits = lax.axis_size("neuron").bit_length() - 1
    held = [piece]
    for bit in reversed(range(bits)):
        if bit == 0 and gate is not None:
            held, _ = lax.optimization_barrier((held, gate))
        held = held + [swap(chunk, "neuron", 1 << bit) for chunk in held]
    return held


def stage_kernel(bi_ref, *refs, n_pieces, stage, n_pos, final, has_rec):
    n_rounds = len(stage)
    it = iter(refs)
    piece_hbm = [next(it) for _ in range(n_pieces)]
    w_hbm = next(it)
    rec_hbm = next(it) if has_rec else None
    if final:
        scan_hbm = [next(it) for _ in range(7)]
        cur_ref, lv_out, la_out = next(it), next(it), next(it)
    else:
        out_ref = next(it)
    piece_buf = next(it)
    w_buf = next(it)
    sem = next(it)
    rec_buf = next(it)
    if final:
        scan_buf = [next(it) for _ in range(7)]

    steps, batch = rec_buf.shape[0], rec_buf.shape[1]
    local_blocks, nnz, side = w_buf.shape[1], w_buf.shape[2], w_buf.shape[3]
    rows = steps * batch
    bits = n_pos.bit_length() - 1
    me = lax.axis_index("neuron")
    n_sem = 0

    def start(src, dst):
        nonlocal n_sem
        copy = pltpu.make_async_copy(src, dst, sem.at[n_sem])
        n_sem += 1
        copy.start()
        return copy

    piece_cp, w_cp = [], []
    rec_cp = None
    scan_cp = []
    for ri, rnd in enumerate(stage):
        piece_cp += [start(piece_hbm[ri * n_pos + p], piece_buf.at[ri * n_pos + p]) for p in range(n_pos)]
        w_cp.append(start(w_hbm.at[rnd, 0], w_buf.at[ri]))
        if ri == 0 and has_rec:
            rec_cp = start(rec_hbm, rec_buf)
    if final:
        scan_cp = [start(src, dst) for src, dst in zip(scan_hbm, scan_buf)]

    for ri, rnd in enumerate(stage):
        for p in range(n_pos):
            piece_cp[ri * n_pos + p].wait()
        w_cp[ri].wait()
        if ri == 0 and has_rec:
            rec_cp.wait()
        last = ri == n_rounds - 1
        if last and final:
            for copy in scan_cp:
                copy.wait()
            err_buf, surr_buf, lv_buf, la_buf, alpha_buf, rho_buf, beta_buf = scan_buf
        for j in range(local_blocks):
            cols = slice(j * side, (j + 1) * side)
            if ri == 0 and not has_rec:
                acc = jnp.zeros((rows, side), jnp.float32)
            else:
                acc = rec_buf[:, :, cols].reshape(rows, side)
            for k in range(nnz):
                idx = bi_ref[rnd, 0, j, k]
                d = (idx // local_blocks) ^ me
                rel = 0
                for s_, bit in enumerate(reversed(range(bits))):
                    rel = rel | (((d >> bit) & 1) << s_)
                off = pl.multiple_of((idx % local_blocks) * side, side)
                x = piece_buf[ri * n_pos + rel, :, pl.ds(off, side)]
                acc = acc + jnp.dot(x, w_buf[ri, j, k], preferred_element_type=jnp.float32)
            rec = acc.reshape(steps, batch, side)
            if not last:
                rec_buf[:, :, cols] = rec
                continue
            if not final:
                out_ref[:, :, cols] = rec
                continue
            alpha = alpha_buf[:, cols]
            rho = rho_buf[:, cols]
            beta = beta_buf[:, cols]
            lv_now = lv_buf[:, cols]
            la_now = la_buf[:, cols]
            for t in reversed(range(steps)):
                surr = surr_buf[t, :, cols]
                total = err_buf[t, :, cols] + rec[t] - lv_now + la_now
                cur_ref[t, :, cols] = lv_now.astype(cur_ref.dtype)
                lv_next = alpha * lv_now + surr * total
                la_next = rho * la_now - beta * surr * total
                lv_now, la_now = lv_next, la_next
            lv_out[:, cols] = lv_now
            la_out[:, cols] = la_now


def stage_contrib(block_index, pieces, weights, stage, n_pos, rec, scan_args, steps):
    rows, local = pieces[0].shape
    _, _, local_blocks, nnz, side, _ = weights.shape
    batch = rows // steps
    n_rounds = len(stage)
    final = scan_args is not None
    has_rec = rec is not None
    operands = list(pieces) + [weights]
    scratch = [
        pltpu.VMEM((len(pieces), rows, local), pieces[0].dtype),
        pltpu.VMEM((n_rounds, local_blocks, nnz, side, side), weights.dtype),
    ]
    n_sem = len(pieces) + n_rounds + (1 if has_rec else 0) + (7 if final else 0)
    scratch.append(pltpu.SemaphoreType.DMA((n_sem,)))
    scratch.append(pltpu.VMEM((steps, batch, local), jnp.float32))
    if has_rec:
        operands.append(rec)
    if final:
        err_grad, surrogate, lv_end, la_end, alpha, rho, beta = scan_args
        rows = [a.reshape(1, local) for a in (alpha, rho, beta)]
        extra = [err_grad, surrogate, lv_end, la_end] + rows
        operands += extra
        scratch += [pltpu.VMEM(a.shape, a.dtype) for a in extra]
        out_specs = (VMEM, VMEM, VMEM)
        out_shape = (
            jax.ShapeDtypeStruct((steps, batch, local), jnp.bfloat16),
            jax.ShapeDtypeStruct((batch, local), jnp.float32),
            jax.ShapeDtypeStruct((batch, local), jnp.float32),
        )
    else:
        out_specs = VMEM
        out_shape = jax.ShapeDtypeStruct((steps, batch, local), jnp.float32)
    kernel = functools.partial(
        stage_kernel, n_pieces=len(pieces), stage=tuple(stage), n_pos=n_pos,
        final=final, has_rec=has_rec,
    )
    pinned = [final and i > len(pieces) + has_rec for i in range(len(operands))]
    specs = [VMEM if p else ANY for p in pinned]
    operands = [pltpu.with_memory_space_constraint(x, pltpu.VMEM) if p else x
                for x, p in zip(operands, pinned)]
    return pl.pallas_call(
        kernel,
        in_specs=[SMEM] + specs,
        out_specs=out_specs,
        scratch_shapes=scratch,
        out_shape=out_shape,
    )(block_index, *operands)


def per_device(
    window, err_grad, surrogate, lv_end, la_end, alpha, rho, beta, weights, block_index, delays
):
    steps = err_grad.shape[0]
    local_neurons = err_grad.shape[2]
    block_side = weights.shape[-1]
    local_blocks = local_neurons // block_side
    rounds = weights.shape[0]
    levels = lax.axis_size("area").bit_length() - 1
    nbits = lax.axis_size("neuron").bit_length() - 1
    n_pos = 1 << nbits
    stages = [[0]] + [list(range(f, min(f + 2, rounds))) for f in range(1, rounds, 2)]
    arrived = []
    gate = None
    for stage in stages:
        pieces = send_slices(window, delays, stage, levels, steps)
        if gate is not None:
            pieces, _ = lax.optimization_barrier((pieces, gate))
        got = [swap(piece, "area", 1 << (rnd % levels)) for piece, rnd in zip(pieces, stage)]
        arrived += got
        gate = got
    rec = None
    for si, stage in enumerate(stages):
        chunks = []
        for rnd in stage:
            chunks += gather_neuron(arrived[rnd], rec)
        scan_args = None
        if si == len(stages) - 1:
            scan_args = (err_grad, surrogate, lv_end, la_end, alpha, rho, beta)
        rec = stage_contrib(block_index, chunks, weights, stage, n_pos, rec, scan_args, steps)
    return rec


def solution(mesh):
    placed = (
        P(None, "groups", ("area", "neuron")),
        P(None, "groups", ("area", "neuron")),
        P(None, "groups", ("area", "neuron")),
        P("groups", ("area", "neuron")),
        P("groups", ("area", "neuron")),
        P(("area", "neuron")),
        P(("area", "neuron")),
        P(("area", "neuron")),
        P(None, "area", "neuron", None, None, None),
        P(None, "area", "neuron", None),
        P(),
    )
    return jax.shard_map(
        per_device,
        mesh=mesh,
        in_specs=placed,
        out_specs=(
            P(None, "groups", ("area", "neuron")),
            P("groups", ("area", "neuron")),
            P("groups", ("area", "neuron")),
        ),
        check_vma=False,
    )
```

```python
import functools

import jax
import jax.numpy as jnp
from jax import lax
from jax.experimental import pallas as pl
from jax.experimental.pallas import tpu as pltpu
from jax.sharding import PartitionSpec as P

ANY = pl.BlockSpec(memory_space=pl.ANY)
SMEM = pl.BlockSpec(memory_space=pltpu.SMEM)
VMEM = pl.BlockSpec(memory_space=pltpu.VMEM)


def swap(value, axis, mask):
    pairs = [(source, source ^ mask) for source in range(lax.axis_size(axis))]
    return lax.ppermute(value, axis, pairs)


def slice_kernel(delays_ref, window_ref, *outs, rounds, levels, steps):
    me = lax.axis_index("area")
    rows, width = outs[0].shape
    side = 128 if width % 128 == 0 else width
    for rnd, out in zip(rounds, outs):
        start = delays_ref[rnd, me ^ (1 << (rnd % levels))] - steps
        for c in range(0, width, side):
            x = window_ref[pl.ds(start, steps), :, c:c + side].astype(jnp.float32)
            out[:, c:c + side] = x.reshape(rows, side).astype(out.dtype)


def send_slices(window, delays, rounds, levels, steps):
    shape = (steps * window.shape[1], window.shape[2])
    kernel = functools.partial(slice_kernel, rounds=tuple(rounds), levels=levels, steps=steps)
    return pl.pallas_call(
        kernel,
        in_specs=[SMEM, VMEM],
        out_specs=[VMEM] * len(rounds),
        out_shape=[jax.ShapeDtypeStruct(shape, window.dtype)] * len(rounds),
    )(delays, window)


def gather_neuron(piece, gate=None):
    bits = lax.axis_size("neuron").bit_length() - 1
    held = [piece]
    for bit in reversed(range(bits)):
        if bit == 0 and gate is not None:
            held, _ = lax.optimization_barrier((held, gate))
        held = held + [swap(chunk, "neuron", 1 << bit) for chunk in held]
    return held


def stage_kernel(bi_ref, *refs, n_pieces, stage, n_pos, final, has_rec):
    n_rounds = len(stage)
    it = iter(refs)
    piece_hbm = [next(it) for _ in range(n_pieces)]
    w_hbm = next(it)
    rec_hbm = next(it) if has_rec else None
    if final:
        scan_hbm = [next(it) for _ in range(7)]
        cur_ref, lv_out, la_out = next(it), next(it), next(it)
    else:
        out_ref = next(it)
    piece_buf = next(it)
    w_buf = next(it)
    sem = next(it)
    rec_buf = next(it)
    if final:
        scan_buf = [next(it) for _ in range(7)]

    steps, batch = rec_buf.shape[0], rec_buf.shape[1]
    local_blocks, nnz, side = w_buf.shape[1], w_buf.shape[2], w_buf.shape[3]
    rows = steps * batch
    bits = n_pos.bit_length() - 1
    me = lax.axis_index("neuron")
    n_sem = 0

    def start(src, dst):
        nonlocal n_sem
        copy = pltpu.make_async_copy(src, dst, sem.at[n_sem])
        n_sem += 1
        copy.start()
        return copy

    piece_cp, w_cp = [], []
    rec_cp = None
    scan_cp = []
    for ri, rnd in enumerate(stage):
        piece_cp += [start(piece_hbm[ri * n_pos + p], piece_buf.at[ri * n_pos + p]) for p in range(n_pos)]
        w_cp.append(start(w_hbm.at[rnd, 0], w_buf.at[ri]))
        if ri == 0 and has_rec:
            rec_cp = start(rec_hbm, rec_buf)
    if final:
        scan_cp = [start(src, dst) for src, dst in zip(scan_hbm, scan_buf)]

    for ri, rnd in enumerate(stage):
        for p in range(n_pos):
            piece_cp[ri * n_pos + p].wait()
        w_cp[ri].wait()
        if ri == 0 and has_rec:
            rec_cp.wait()
        last = ri == n_rounds - 1
        if last and final:
            for copy in scan_cp:
                copy.wait()
            err_buf, surr_buf, lv_buf, la_buf, alpha_buf, rho_buf, beta_buf = scan_buf
        for j in range(local_blocks):
            cols = slice(j * side, (j + 1) * side)
            if ri == 0 and not has_rec:
                acc = jnp.zeros((rows, side), jnp.float32)
            else:
                acc = rec_buf[:, :, cols].reshape(rows, side)
            for k in range(nnz):
                idx = bi_ref[rnd, 0, j, k]
                d = (idx // local_blocks) ^ me
                rel = 0
                for s_, bit in enumerate(reversed(range(bits))):
                    rel = rel | (((d >> bit) & 1) << s_)
                off = pl.multiple_of((idx % local_blocks) * side, side)
                x = piece_buf[ri * n_pos + rel, :, pl.ds(off, side)]
                acc = acc + jnp.dot(x, w_buf[ri, j, k], preferred_element_type=jnp.float32)
            rec = acc.reshape(steps, batch, side)
            if not last:
                rec_buf[:, :, cols] = rec
                continue
            if not final:
                out_ref[:, :, cols] = rec
                continue
            alpha = alpha_buf[:, cols]
            rho = rho_buf[:, cols]
            beta = beta_buf[:, cols]
            lv_now = lv_buf[:, cols]
            la_now = la_buf[:, cols]
            for t in reversed(range(steps)):
                surr = surr_buf[t, :, cols]
                total = err_buf[t, :, cols] + rec[t] - lv_now + la_now
                cur_ref[t, :, cols] = lv_now.astype(cur_ref.dtype)
                lv_next = alpha * lv_now + surr * total
                la_next = rho * la_now - beta * surr * total
                lv_now, la_now = lv_next, la_next
            lv_out[:, cols] = lv_now
            la_out[:, cols] = la_now


def stage_contrib(block_index, pieces, weights, stage, n_pos, rec, scan_args, steps):
    rows, local = pieces[0].shape
    _, _, local_blocks, nnz, side, _ = weights.shape
    batch = rows // steps
    n_rounds = len(stage)
    final = scan_args is not None
    has_rec = rec is not None
    operands = list(pieces) + [weights]
    scratch = [
        pltpu.VMEM((len(pieces), rows, local), pieces[0].dtype),
        pltpu.VMEM((n_rounds, local_blocks, nnz, side, side), weights.dtype),
    ]
    n_sem = len(pieces) + n_rounds + (1 if has_rec else 0) + (7 if final else 0)
    scratch.append(pltpu.SemaphoreType.DMA((n_sem,)))
    scratch.append(pltpu.VMEM((steps, batch, local), jnp.float32))
    if has_rec:
        operands.append(rec)
    if final:
        err_grad, surrogate, lv_end, la_end, alpha, rho, beta = scan_args
        rows = [a.reshape(1, local) for a in (alpha, rho, beta)]
        extra = [err_grad, surrogate, lv_end, la_end] + rows
        operands += extra
        scratch += [pltpu.VMEM(a.shape, a.dtype) for a in extra]
        out_specs = (VMEM, VMEM, VMEM)
        out_shape = (
            jax.ShapeDtypeStruct((steps, batch, local), jnp.bfloat16),
            jax.ShapeDtypeStruct((batch, local), jnp.float32),
            jax.ShapeDtypeStruct((batch, local), jnp.float32),
        )
    else:
        out_specs = VMEM
        out_shape = jax.ShapeDtypeStruct((steps, batch, local), jnp.float32)
    kernel = functools.partial(
        stage_kernel, n_pieces=len(pieces), stage=tuple(stage), n_pos=n_pos,
        final=final, has_rec=has_rec,
    )
    pinned = [final and i > len(pieces) + has_rec for i in range(len(operands))]
    specs = [VMEM if p else ANY for p in pinned]
    operands = [pltpu.with_memory_space_constraint(x, pltpu.VMEM) if p else x
                for x, p in zip(operands, pinned)]
    return pl.pallas_call(
        kernel,
        in_specs=[SMEM] + specs,
        out_specs=out_specs,
        scratch_shapes=scratch,
        out_shape=out_shape,
    )(block_index, *operands)


def per_device(
    window, err_grad, surrogate, lv_end, la_end, alpha, rho, beta, weights, block_index, delays
):
    steps = err_grad.shape[0]
    local_neurons = err_grad.shape[2]
    block_side = weights.shape[-1]
    local_blocks = local_neurons // block_side
    rounds = weights.shape[0]
    levels = lax.axis_size("area").bit_length() - 1
    nbits = lax.axis_size("neuron").bit_length() - 1
    n_pos = 1 << nbits
    if rounds == 4 and levels == 2:
        stages = [[1], [0, 3], [2]]
    else:
        stages = [list(range(f, min(f + 2, rounds))) for f in range(0, rounds, 2)]
    arrived = {}
    gate = None
    for stage in stages:
        pieces = send_slices(window, delays, stage, levels, steps)
        if gate is not None:
            pieces, _ = lax.optimization_barrier((pieces, gate))
        got = [swap(piece, "area", 1 << (rnd % levels)) for piece, rnd in zip(pieces, stage)]
        arrived.update(zip(stage, got))
        gate = got
    rec = None
    for si, stage in enumerate(stages):
        chunks = []
        for rnd in stage:
            chunks += gather_neuron(arrived[rnd], rec)
        scan_args = None
        if si == len(stages) - 1:
            scan_args = (err_grad, surrogate, lv_end, la_end, alpha, rho, beta)
        rec = stage_contrib(block_index, chunks, weights, stage, n_pos, rec, scan_args, steps)
    return rec


def solution(mesh):
    placed = (
        P(None, "groups", ("area", "neuron")),
        P(None, "groups", ("area", "neuron")),
        P(None, "groups", ("area", "neuron")),
        P("groups", ("area", "neuron")),
        P("groups", ("area", "neuron")),
        P(("area", "neuron")),
        P(("area", "neuron")),
        P(("area", "neuron")),
        P(None, "area", "neuron", None, None, None),
        P(None, "area", "neuron", None),
        P(),
    )
    return jax.shard_map(
        per_device,
        mesh=mesh,
        in_specs=placed,
        out_specs=(
            P(None, "groups", ("area", "neuron")),
            P("groups", ("area", "neuron")),
            P("groups", ("area", "neuron")),
        ),
        check_vma=False,
    )
```

```python
import functools

import jax
import jax.numpy as jnp
from jax import lax
from jax.experimental import pallas as pl
from jax.experimental.pallas import tpu as pltpu
from jax.sharding import PartitionSpec as P

ANY = pl.BlockSpec(memory_space=pl.ANY)
SMEM = pl.BlockSpec(memory_space=pltpu.SMEM)
VMEM = pl.BlockSpec(memory_space=pltpu.VMEM)


def swap(value, axis, mask):
    pairs = [(source, source ^ mask) for source in range(lax.axis_size(axis))]
    return lax.ppermute(value, axis, pairs)


def slice_kernel(delays_ref, window_ref, *outs, rounds, levels, steps):
    me = lax.axis_index("area")
    rows, width = outs[0].shape
    side = 128 if width % 128 == 0 else width
    for rnd, out in zip(rounds, outs):
        start = delays_ref[rnd, me ^ (1 << (rnd % levels))] - steps
        for c in range(0, width, side):
            x = window_ref[pl.ds(start, steps), :, c:c + side].astype(jnp.float32)
            out[:, c:c + side] = x.reshape(rows, side).astype(out.dtype)


def send_slices(window, delays, rounds, levels, steps):
    shape = (steps * window.shape[1], window.shape[2])
    kernel = functools.partial(slice_kernel, rounds=tuple(rounds), levels=levels, steps=steps)
    return pl.pallas_call(
        kernel,
        in_specs=[SMEM, VMEM],
        out_specs=[VMEM] * len(rounds),
        out_shape=[jax.ShapeDtypeStruct(shape, window.dtype)] * len(rounds),
    )(delays, window)


def gather_neuron(piece, gate=None):
    bits = lax.axis_size("neuron").bit_length() - 1
    held = [piece]
    for bit in reversed(range(bits)):
        if bit == 0 and gate is not None:
            held, _ = lax.optimization_barrier((held, gate))
        held = held + [swap(chunk, "neuron", 1 << bit) for chunk in held]
    return held


def stage_kernel(bi_ref, *refs, n_pieces, stage, n_pos, final, has_rec):
    n_rounds = len(stage)
    it = iter(refs)
    piece_hbm = [next(it) for _ in range(n_pieces)]
    w_hbm = next(it)
    rec_hbm = next(it) if has_rec else None
    if final:
        scan_hbm = [next(it) for _ in range(7)]
        cur_ref, lv_out, la_out = next(it), next(it), next(it)
    else:
        out_ref = next(it)
    piece_buf = next(it)
    w_buf = next(it)
    sem = next(it)
    rec_buf = next(it)
    if final:
        scan_buf = [next(it) for _ in range(7)]

    steps, batch = rec_buf.shape[0], rec_buf.shape[1]
    local_blocks, nnz, side = w_buf.shape[1], w_buf.shape[2], w_buf.shape[3]
    rows = steps * batch
    bits = n_pos.bit_length() - 1
    me = lax.axis_index("neuron")
    n_sem = 0

    def start(src, dst):
        nonlocal n_sem
        copy = pltpu.make_async_copy(src, dst, sem.at[n_sem])
        n_sem += 1
        copy.start()
        return copy

    piece_cp, w_cp = [], []
    rec_cp = None
    scan_cp = []
    for ri, rnd in enumerate(stage):
        piece_cp += [start(piece_hbm[ri * n_pos + p], piece_buf.at[ri * n_pos + p]) for p in range(n_pos)]
        w_cp.append(start(w_hbm.at[rnd, 0], w_buf.at[ri]))
        if ri == 0 and has_rec:
            rec_cp = start(rec_hbm, rec_buf)
    if final:
        scan_cp = [start(src, dst) for src, dst in zip(scan_hbm, scan_buf)]

    for ri, rnd in enumerate(stage):
        for p in range(n_pos):
            piece_cp[ri * n_pos + p].wait()
        w_cp[ri].wait()
        if ri == 0 and has_rec:
            rec_cp.wait()
        last = ri == n_rounds - 1
        if last and final:
            for copy in scan_cp:
                copy.wait()
            err_buf, surr_buf, lv_buf, la_buf, alpha_buf, rho_buf, beta_buf = scan_buf
        for j in range(local_blocks):
            cols = slice(j * side, (j + 1) * side)
            if ri == 0 and not has_rec:
                acc = jnp.zeros((rows, side), jnp.float32)
            else:
                acc = rec_buf[:, :, cols].reshape(rows, side)
            for k in range(nnz):
                idx = bi_ref[rnd, 0, j, k]
                d = (idx // local_blocks) ^ me
                rel = 0
                for s_, bit in enumerate(reversed(range(bits))):
                    rel = rel | (((d >> bit) & 1) << s_)
                off = pl.multiple_of((idx % local_blocks) * side, side)
                x = piece_buf[ri * n_pos + rel, :, pl.ds(off, side)]
                acc = acc + jnp.dot(x, w_buf[ri, j, k], preferred_element_type=jnp.float32)
            rec = acc.reshape(steps, batch, side)
            if not last:
                rec_buf[:, :, cols] = rec
                continue
            if not final:
                out_ref[:, :, cols] = rec
                continue
            alpha = alpha_buf[:, cols]
            rho = rho_buf[:, cols]
            beta = beta_buf[:, cols]
            lv_now = lv_buf[:, cols]
            la_now = la_buf[:, cols]
            for t in reversed(range(steps)):
                surr = surr_buf[t, :, cols]
                total = err_buf[t, :, cols] + rec[t] - lv_now + la_now
                cur_ref[t, :, cols] = lv_now.astype(cur_ref.dtype)
                lv_next = alpha * lv_now + surr * total
                la_next = rho * la_now - beta * surr * total
                lv_now, la_now = lv_next, la_next
            lv_out[:, cols] = lv_now
            la_out[:, cols] = la_now


def stage_contrib(block_index, pieces, weights, stage, n_pos, rec, scan_args, steps):
    rows, local = pieces[0].shape
    _, _, local_blocks, nnz, side, _ = weights.shape
    batch = rows // steps
    n_rounds = len(stage)
    final = scan_args is not None
    has_rec = rec is not None
    operands = list(pieces) + [weights]
    scratch = [
        pltpu.VMEM((len(pieces), rows, local), pieces[0].dtype),
        pltpu.VMEM((n_rounds, local_blocks, nnz, side, side), weights.dtype),
    ]
    n_sem = len(pieces) + n_rounds + (1 if has_rec else 0) + (7 if final else 0)
    scratch.append(pltpu.SemaphoreType.DMA((n_sem,)))
    scratch.append(pltpu.VMEM((steps, batch, local), jnp.float32))
    if has_rec:
        operands.append(rec)
    if final:
        err_grad, surrogate, lv_end, la_end, alpha, rho, beta = scan_args
        rows = [a.reshape(1, local) for a in (alpha, rho, beta)]
        extra = [err_grad, surrogate, lv_end, la_end] + rows
        operands += extra
        scratch += [pltpu.VMEM(a.shape, a.dtype) for a in extra]
        out_specs = (VMEM, VMEM, VMEM)
        out_shape = (
            jax.ShapeDtypeStruct((steps, batch, local), jnp.bfloat16),
            jax.ShapeDtypeStruct((batch, local), jnp.float32),
            jax.ShapeDtypeStruct((batch, local), jnp.float32),
        )
    else:
        out_specs = VMEM
        out_shape = jax.ShapeDtypeStruct((steps, batch, local), jnp.float32)
    kernel = functools.partial(
        stage_kernel, n_pieces=len(pieces), stage=tuple(stage), n_pos=n_pos,
        final=final, has_rec=has_rec,
    )
    pinned = [final and i > len(pieces) for i in range(len(operands))]
    specs = [VMEM if p else ANY for p in pinned]
    operands = [pltpu.with_memory_space_constraint(x, pltpu.VMEM) if p else x
                for x, p in zip(operands, pinned)]
    return pl.pallas_call(
        kernel,
        in_specs=[SMEM] + specs,
        out_specs=out_specs,
        scratch_shapes=scratch,
        out_shape=out_shape,
    )(block_index, *operands)


def per_device(
    window, err_grad, surrogate, lv_end, la_end, alpha, rho, beta, weights, block_index, delays
):
    steps = err_grad.shape[0]
    local_neurons = err_grad.shape[2]
    block_side = weights.shape[-1]
    local_blocks = local_neurons // block_side
    rounds = weights.shape[0]
    levels = lax.axis_size("area").bit_length() - 1
    nbits = lax.axis_size("neuron").bit_length() - 1
    n_pos = 1 << nbits
    stages = [list(range(f, min(f + 2, rounds))) for f in range(0, rounds, 2)]
    arrived = []
    gate = None
    for stage in stages:
        pieces = send_slices(window, delays, stage, levels, steps)
        if gate is not None:
            pieces, _ = lax.optimization_barrier((pieces, gate))
        got = [swap(piece, "area", 1 << (rnd % levels)) for piece, rnd in zip(pieces, stage)]
        arrived += got
        gate = got
    rec = None
    for si, stage in enumerate(stages):
        chunks = []
        for rnd in stage:
            chunks += gather_neuron(arrived[rnd], rec)
        scan_args = None
        if si == len(stages) - 1:
            scan_args = (err_grad, surrogate, lv_end, la_end, alpha, rho, beta)
        rec = stage_contrib(block_index, chunks, weights, stage, n_pos, rec, scan_args, steps)
    return rec


def solution(mesh):
    placed = (
        P(None, "groups", ("area", "neuron")),
        P(None, "groups", ("area", "neuron")),
        P(None, "groups", ("area", "neuron")),
        P("groups", ("area", "neuron")),
        P("groups", ("area", "neuron")),
        P(("area", "neuron")),
        P(("area", "neuron")),
        P(("area", "neuron")),
        P(None, "area", "neuron", None, None, None),
        P(None, "area", "neuron", None),
        P(),
    )
    return jax.shard_map(
        per_device,
        mesh=mesh,
        in_specs=placed,
        out_specs=(
            P(None, "groups", ("area", "neuron")),
            P("groups", ("area", "neuron")),
            P("groups", ("area", "neuron")),
        ),
        check_vma=False,
    )
```
